32 devices in a mesh: grp: 2 (over y), ctx: 4 (over z), head: 4 (over x, core).
Axes of the slice: x: 2, y: 2, z: 4, core: 2. Of those that a mesh axis runs over, the one named last changes fastest.
Arguments:
- queries: bfloat16 [512, 8192], P(('grp', 'ctx'), 'head'), parts along dimension 0
- latents: bfloat16 [512, 320], P(('grp', 'ctx')), parts along dimension 0
- w_kv_up: bfloat16 [256, 8192], P(None, 'head'), may hold values from -0.375 to 0.375
- w_out: bfloat16 [4096, 7168], P('head', 'ctx'), may hold values from -0.125 to 0.125
- block_order: int32 [16], P('grp'), parts along dimension 0, may hold values from 0 to 7, each once
Outputs:
- attended: bfloat16 [512, 7168], P(('grp', 'head'), 'ctx'), parts along dimension 0
The draws below stay inside these ranges and needn't reach their ends.
There are 2 independent parts, one for each index of `grp`. The reference program is written for one: setup_inputs(seed, part) draws one part's arguments, and reference() takes and returns one part's arrays. A program takes and returns all parts, laid end to end along the dimension named above; an argument that names none is the same for every part. Nothing has to cross between parts.
Inputs may be any that keep to these rules, and one draw needn't show every extreme that they name: block_order lists each of the 8 sequence blocks once.
All inputs are finite; a program needn't handle non-finite values.
Results may differ from the reference program's by a relative error of at most 0.011.
Values may be sent and summed in bfloat16 or wider, within the bound.
No kernel may reach another device: no remote copies, remote signals or barrier semaphores. Data moves between devices by JAX's collectives and lax.ppermute only.
A program may use at most 128 MiB of HBM per device.

```python
import math
import jax
import jax.numpy as jnp
from jax import lax

D = 7168
LATENT = 256
ROPE = 64
HEAD_DIM = 64
V_DIM = 64
HEADS_DEV = 16
HALF = 32
BLOCKS = 8
TOKENS = 256
HEADS = 64


def shared_draw(key):
    base = jax.random.fold_in(key, 7)
    keys = jax.random.split(base, 3)
    width_qk = HEAD_DIM + ROPE
    latent_part = jnp.clip(jax.random.normal(keys[0], (TOKENS, LATENT), jnp.float32), -4.5, 4.5)
    rotary = jnp.clip(jax.random.normal(keys[1], (TOKENS, ROPE), jnp.float32), -4.5, 4.5)
    query_all = jnp.clip(1.5 * jax.random.normal(keys[2], (TOKENS, HEADS, width_qk), jnp.float32), -6.0, 6.0)
    return (latent_part, rotary, query_all.reshape(TOKENS, HEADS * width_qk))


def draw_queries(key, part):
    return shared_draw(key)[2].astype(jnp.bfloat16)


def draw_latents(key, part):
    latent_part, rotary, query_all = shared_draw(key)
    return jnp.concatenate([latent_part, rotary], axis=1).astype(jnp.bfloat16)


def block_scale(rng, extent, cuts, smallest, largest):
    def one(dim, parts):
        draws = jax.random.uniform(jax.random.fold_in(jax.random.fold_in(rng, 6), dim), (parts,), jnp.float32, smallest / len(cuts), largest / len(cuts))
        return jnp.repeat(jnp.exp(draws), extent[dim] // parts).reshape((-1,) + (1,) * (len(extent) - dim - 1))

    gain = one(*cuts[0])
    for cut in cuts[1:]:
        gain = gain * one(*cut)
    return gain


def normal_values(stream_key, shape, deviation, most, cuts=(), kind=jnp.bfloat16):
    entries = deviation * jax.random.normal(stream_key, shape, jnp.float32)
    if cuts:
        entries = entries * block_scale(stream_key, shape, cuts, -0.22, 0.18)
    return jnp.clip(entries, -most, most).astype(kind)


def setup_inputs(seed: int = 0, part: int = 0) -> dict:
    streams_of = jax.random.split(jax.random.key(seed), 6)
    own_keys = jax.random.split(jax.random.fold_in(streams_of[5], part), 6)
    return {
        "queries": draw_queries(jax.random.fold_in(jax.random.fold_in(streams_of[5], part), 71), part),
        "latents": draw_latents(jax.random.fold_in(jax.random.fold_in(streams_of[5], part), 71), part),
        "w_kv_up": normal_values(streams_of[2], (LATENT, HEADS * (HEAD_DIM + V_DIM)), LATENT ** -0.5, 0.375, ((1, 4),)),
        "w_out": normal_values(streams_of[3], (HEADS * V_DIM, D), (2 * V_DIM * HEADS_DEV) ** -0.5, 0.125, ((0, 4), (1, 4))),
        "block_order": jax.random.permutation(own_keys[4], BLOCKS).astype(jnp.int32),
    }


def reference(queries, latents, w_kv_up, w_out, block_order):
    width_qk = HEAD_DIM + ROPE
    scale = 1.0 / math.sqrt(width_qk)
    rows_all = jnp.arange(TOKENS, dtype=jnp.int32)
    position = block_order[rows_all // HALF] * HALF + rows_all % HALF
    latent_part = latents[:, :LATENT]
    rotary = latents[:, LATENT:]
    query_heads = queries.reshape(TOKENS, HEADS, width_qk).transpose(1, 0, 2)
    weight_heads = w_kv_up.reshape(LATENT, HEADS, HEAD_DIM + V_DIM).transpose(1, 0, 2)
    block_rows = math.gcd(TOKENS, 512)
    highest_p = lax.Precision.HIGHEST

    def one_head(pair):
        query_one, weight_one = pair
        packed = jnp.dot(latent_part, weight_one, preferred_element_type=jnp.float32)
        key_nope = packed[:, :HEAD_DIM]
        values = packed[:, HEAD_DIM:]
        query_blocks = query_one.reshape(TOKENS // block_rows, block_rows, width_qk)
        pos_blocks = position.reshape(TOKENS // block_rows, block_rows)

        def one_block(inner):
            query_rows, query_pos = inner
            scores = jnp.dot(query_rows[:, :HEAD_DIM].astype(jnp.float32), key_nope.T, precision=highest_p)
            scores = scores + jnp.dot(query_rows[:, HEAD_DIM:], rotary.T, preferred_element_type=jnp.float32)
            scores = scores * scale
            visible = position[None, :] <= query_pos[:, None]
            scores = jnp.where(visible, scores, -1e+30)
            highest = lax.optimization_barrier(jnp.max(scores, axis=1, keepdims=True))
            weights = jnp.where(visible, jnp.exp(scores - highest), 0.0)
            totals = lax.optimization_barrier(jnp.sum(weights, axis=1, keepdims=True))
            rounded = lax.optimization_barrier(weights.astype(jnp.bfloat16)).astype(jnp.float32)
            mixed = jnp.dot(rounded, values, precision=highest_p)
            return (mixed / totals).astype(jnp.bfloat16)
        return lax.map(one_block, (query_blocks, pos_blocks)).reshape(TOKENS, V_DIM)
    outputs = lax.map(one_head, (query_heads, weight_heads))
    outputs = outputs.transpose(1, 0, 2).reshape(TOKENS, HEADS * V_DIM)
    return jnp.dot(outputs, w_out, preferred_element_type=jnp.float32).astype(jnp.bfloat16)
```

```python
import math

import jax
import jax.numpy as jnp
from jax import lax
from jax.sharding import PartitionSpec as P

LATENT = 256
ROPE = 64
HEAD_DIM = 64
V_DIM = 64

NEGATIVE = -1e30
DIRECT_LIMIT = 8


def positions_of(block_order, global_rows, half_rows):
    block_index = global_rows // half_rows
    matches = block_index[:, None] == jnp.arange(block_order.shape[0], dtype=jnp.int32)[None, :]
    picked = jnp.sum(jnp.where(matches, block_order[None, :], 0), axis=1)
    return picked * half_rows + global_rows % half_rows


def gather_ctx(x, ctx_size):
    me = lax.axis_index("ctx")
    if ctx_size > DIRECT_LIMIT:
        whole = lax.all_gather(x, "ctx", axis=0, tiled=False)
        return whole, jnp.arange(ctx_size, dtype=jnp.int32)
    pieces = [x]
    for shift in range(1, ctx_size):
        pairs = [(i, (i + shift) % ctx_size) for i in range(ctx_size)]
        pieces.append(lax.ppermute(x, "ctx", pairs))
    sources = (me - jnp.arange(ctx_size, dtype=jnp.int32)) % ctx_size
    return jnp.stack(pieces), sources


def reduce_scatter_head(relative, head_size):
    acc = relative
    bit = 1
    while bit < head_size:
        pairs = [(i, i ^ bit) for i in range(head_size)]
        grouped = acc.reshape((acc.shape[0] // 2, 2) + acc.shape[1:])
        kept = grouped[:, 0]
        sent = grouped[:, 1].astype(jnp.bfloat16)
        got = lax.ppermute(sent, "head", pairs)
        acc = kept + got.astype(jnp.float32)
        bit *= 2
    return acc[0]


def on_device(queries, latents, w_kv_up, w_out, block_order, *, ctx_size, head_size):
    rows_here = queries.shape[0]
    half_rows = rows_here // 2
    width_qk = HEAD_DIM + ROPE
    width_kv = HEAD_DIM + V_DIM
    heads_here = w_kv_up.shape[1] // width_kv
    scaling = 1.0 / math.sqrt(width_qk)
    highest_p = lax.Precision.HIGHEST
    me_ctx = lax.axis_index("ctx")
    me_head = lax.axis_index("head")

    blocks, sources = gather_ctx(latents, ctx_size)
    piece = blocks.reshape(ctx_size * rows_here, latents.shape[1])
    token_rows = (sources[:, None] * rows_here + jnp.arange(rows_here, dtype=jnp.int32)[None, :]).reshape(-1)

    queries3 = queries.reshape(rows_here, heads_here, width_qk)
    query_nope = queries3[:, :, :HEAD_DIM].astype(jnp.float32)
    query_rope = queries3[:, :, HEAD_DIM:]
    query_rows = me_ctx * rows_here + jnp.arange(rows_here, dtype=jnp.int32)
    query_pos = positions_of(block_order, query_rows, half_rows)

    row_count = piece.shape[0]
    packed = jnp.dot(piece[:, :LATENT], w_kv_up, preferred_element_type=jnp.float32)
    packed = packed.reshape(row_count, heads_here, width_kv)
    scores = jnp.einsum("qhd,khd->qhk", query_nope, packed[:, :, :HEAD_DIM], precision=highest_p)
    scores = scores + jnp.einsum(
        "qhd,kd->qhk", query_rope, piece[:, LATENT:], preferred_element_type=jnp.float32
    )
    scores = scores * scaling
    visible = (positions_of(block_order, token_rows, half_rows)[None, :] <= query_pos[:, None])[:, None, :]
    scores = jnp.where(visible, scores, NEGATIVE)
    highest = jnp.max(scores, axis=2, keepdims=True)
    weights = jnp.where(visible, jnp.exp(scores - highest), 0.0)
    totals = jnp.sum(weights, axis=2, keepdims=True)
    widened = lax.optimization_barrier(weights.astype(jnp.bfloat16)).astype(jnp.float32)
    mixed = jnp.einsum("qhk,khd->qhd", widened, packed[:, :, HEAD_DIM:], precision=highest_p)
    outputs = (mixed / totals).astype(jnp.bfloat16).reshape(rows_here, heads_here * V_DIM)

    out_blocks, out_sources = gather_ctx(outputs, ctx_size)
    per_target = ctx_size // head_size
    if ctx_size > DIRECT_LIMIT:
        slot_of_block = jnp.arange(ctx_size, dtype=jnp.int32)
    else:
        slot_of_block = (me_ctx - jnp.arange(ctx_size, dtype=jnp.int32)) % ctx_size
    relative_targets = jnp.arange(head_size, dtype=jnp.int32) ^ me_head
    wanted_blocks = (relative_targets[:, None] * per_target + jnp.arange(per_target, dtype=jnp.int32)[None, :]).reshape(-1)
    ordered = jnp.take(out_blocks, slot_of_block[wanted_blocks], axis=0)
    ordered = ordered.reshape(head_size, per_target * rows_here, heads_here * V_DIM)
    partials = jnp.einsum("trf,fc->trc", ordered, w_out, preferred_element_type=jnp.float32)
    total = reduce_scatter_head(partials, head_size)
    return total.astype(jnp.bfloat16)


def solution(mesh):
    placed = (
        P(("grp", "ctx"), "head"),
        P(("grp", "ctx"), None),
        P(None, "head"),
        P("head", "ctx"),
        P("grp"),
    )
    body = lambda *args: on_device(*args, ctx_size=mesh.shape["ctx"], head_size=mesh.shape["head"])
    return jax.shard_map(
        body, mesh=mesh, in_specs=placed, out_specs=P(("grp", "head"), "ctx"), check_vma=False
    )
```

```python
import math

import jax
import jax.numpy as jnp
from jax import lax
from jax.sharding import PartitionSpec as P

LATENT = 256
ROPE = 64
HEAD_DIM = 64
V_DIM = 64

NEGATIVE = -1e30
DIRECT_LIMIT = 8
CHUNKS = 2


def positions_of(block_order, global_rows, half_rows):
    block_index = global_rows // half_rows
    matches = block_index[:, None] == jnp.arange(block_order.shape[0], dtype=jnp.int32)[None, :]
    picked = jnp.sum(jnp.where(matches, block_order[None, :], 0), axis=1)
    return picked * half_rows + global_rows % half_rows


def gather_ctx(x, ctx_size):
    me = lax.axis_index("ctx")
    if ctx_size > DIRECT_LIMIT:
        whole = lax.all_gather(x, "ctx", axis=0, tiled=False)
        return whole, jnp.arange(ctx_size, dtype=jnp.int32)
    pieces = [x]
    for shift in range(1, ctx_size):
        pairs = [(i, (i + shift) % ctx_size) for i in range(ctx_size)]
        pieces.append(lax.ppermute(x, "ctx", pairs))
    sources = (me - jnp.arange(ctx_size, dtype=jnp.int32)) % ctx_size
    return jnp.stack(pieces), sources


def reduce_scatter_head(relative, head_size):
    acc = relative
    bit = 1
    while bit < head_size:
        pairs = [(i, i ^ bit) for i in range(head_size)]
        grouped = acc.reshape((acc.shape[0] // 2, 2) + acc.shape[1:])
        kept = grouped[:, 0]
        sent = grouped[:, 1].astype(jnp.bfloat16)
        got = lax.ppermute(sent, "head", pairs)
        acc = kept + got.astype(jnp.float32)
        bit *= 2
    return acc[0]


def on_device(queries, latents, w_kv_up, w_out, block_order, *, ctx_size, head_size, chunks):
    rows_here = queries.shape[0]
    half_rows = rows_here // 2
    width_qk = HEAD_DIM + ROPE
    width_kv = HEAD_DIM + V_DIM
    heads_here = w_kv_up.shape[1] // width_kv
    scaling = 1.0 / math.sqrt(width_qk)
    highest_p = lax.Precision.HIGHEST
    me_ctx = lax.axis_index("ctx")
    me_head = lax.axis_index("head")

    blocks, sources = gather_ctx(latents, ctx_size)
    piece = blocks.reshape(ctx_size * rows_here, latents.shape[1])
    token_rows = (sources[:, None] * rows_here + jnp.arange(rows_here, dtype=jnp.int32)[None, :]).reshape(-1)
    key_pos = positions_of(block_order, token_rows, half_rows)

    queries3 = queries.reshape(rows_here, heads_here, width_qk)
    query_rows = me_ctx * rows_here + jnp.arange(rows_here, dtype=jnp.int32)
    query_pos = positions_of(block_order, query_rows, half_rows)

    row_count = piece.shape[0]
    packed = jnp.dot(piece[:, :LATENT], w_kv_up, preferred_element_type=jnp.float32)
    packed = packed.reshape(row_count, heads_here, width_kv)
    keys = packed[:, :, :HEAD_DIM]
    values = packed[:, :, HEAD_DIM:]
    rotary = piece[:, LATENT:]

    per_target = ctx_size // head_size
    if ctx_size > DIRECT_LIMIT:
        slot_of_block = jnp.arange(ctx_size, dtype=jnp.int32)
    else:
        slot_of_block = (me_ctx - jnp.arange(ctx_size, dtype=jnp.int32)) % ctx_size
    relative_targets = jnp.arange(head_size, dtype=jnp.int32) ^ me_head
    wanted_blocks = (relative_targets[:, None] * per_target + jnp.arange(per_target, dtype=jnp.int32)[None, :]).reshape(-1)
    wanted_slots = slot_of_block[wanted_blocks]

    chunk_rows = rows_here // chunks
    results = []
    for chunk in range(chunks):
        rows = slice(chunk * chunk_rows, (chunk + 1) * chunk_rows)
        query_nope = queries3[rows, :, :HEAD_DIM].astype(jnp.float32)
        query_rope = queries3[rows, :, HEAD_DIM:]
        scores = jnp.einsum("qhd,khd->qhk", query_nope, keys, precision=highest_p)
        scores = scores + jnp.einsum("qhd,kd->qhk", query_rope, rotary, preferred_element_type=jnp.float32)
        scores = scores * scaling
        visible = (key_pos[None, :] <= query_pos[rows, None])[:, None, :]
        scores = jnp.where(visible, scores, NEGATIVE)
        highest = jnp.max(scores, axis=2, keepdims=True)
        weights = jnp.where(visible, jnp.exp(scores - highest), 0.0)
        totals = jnp.sum(weights, axis=2, keepdims=True)
        widened = lax.optimization_barrier(weights.astype(jnp.bfloat16)).astype(jnp.float32)
        mixed = jnp.einsum("qhk,khd->qhd", widened, values, precision=highest_p)
        outputs = (mixed / totals).astype(jnp.bfloat16).reshape(chunk_rows, heads_here * V_DIM)

        out_blocks, _ = gather_ctx(outputs, ctx_size)
        ordered = jnp.take(out_blocks, wanted_slots, axis=0)
        ordered = ordered.reshape(head_size, per_target * chunk_rows, heads_here * V_DIM)
        partials = jnp.einsum("trf,fc->trc", ordered, w_out, preferred_element_type=jnp.float32)
        total = reduce_scatter_head(partials, head_size)
        results.append(total.reshape(per_target, chunk_rows, -1))
    joined = jnp.stack(results, axis=1).reshape(per_target * rows_here, -1)
    return joined.astype(jnp.bfloat16)


def solution(mesh):
    placed = (
        P(("grp", "ctx"), "head"),
        P(("grp", "ctx"), None),
        P(None, "head"),
        P("head", "ctx"),
        P("grp"),
    )
    body = lambda *args: on_device(*args, ctx_size=mesh.shape["ctx"], head_size=mesh.shape["head"], chunks=CHUNKS)
    return jax.shard_map(
        body, mesh=mesh, in_specs=placed, out_specs=P(("grp", "head"), "ctx"), check_vma=False
    )
```

```python
import math

import jax
import jax.numpy as jnp
from jax import lax
from jax.sharding import PartitionSpec as P

LATENT = 256
ROPE = 64
HEAD_DIM = 64
V_DIM = 64

NEGATIVE = -1e30
DIRECT_LIMIT = 8
CHUNKS = 2


def positions_of(block_order, global_rows, half_rows):
    block_index = global_rows // half_rows
    matches = block_index[:, None] == jnp.arange(block_order.shape[0], dtype=jnp.int32)[None, :]
    picked = jnp.sum(jnp.where(matches, block_order[None, :], 0), axis=1)
    return picked * half_rows + global_rows % half_rows


def gather_ctx(x, ctx_size):
    me = lax.axis_index("ctx")
    if ctx_size > DIRECT_LIMIT:
        whole = lax.all_gather(x, "ctx", axis=0, tiled=False)
        return whole, jnp.arange(ctx_size, dtype=jnp.int32)
    pieces = [x]
    for shift in range(1, ctx_size):
        pairs = [(i, (i + shift) % ctx_size) for i in range(ctx_size)]
        pieces.append(lax.ppermute(x, "ctx", pairs))
    sources = (me - jnp.arange(ctx_size, dtype=jnp.int32)) % ctx_size
    return jnp.stack(pieces), sources


def reduce_scatter_head(relative, head_size):
    acc = relative
    bit = 1
    while bit < head_size:
        pairs = [(i, i ^ bit) for i in range(head_size)]
        grouped = acc.reshape((acc.shape[0] // 2, 2) + acc.shape[1:])
        kept = grouped[:, 0]
        sent = grouped[:, 1].astype(jnp.bfloat16)
        got = lax.ppermute(sent, "head", pairs)
        acc = kept + got.astype(jnp.float32)
        bit *= 2
    return acc[0]


def on_device(queries, latents, w_kv_up, w_out, block_order, *, ctx_size, head_size, chunks):
    rows_here = queries.shape[0]
    half_rows = rows_here // 2
    width_qk = HEAD_DIM + ROPE
    width_kv = HEAD_DIM + V_DIM
    heads_here = w_kv_up.shape[1] // width_kv
    scaling = 1.0 / math.sqrt(width_qk)
    highest_p = lax.Precision.HIGHEST
    me_ctx = lax.axis_index("ctx")
    me_head = lax.axis_index("head")

    blocks, sources = gather_ctx(latents, ctx_size)
    piece = blocks.reshape(ctx_size * rows_here, latents.shape[1])
    token_rows = (sources[:, None] * rows_here + jnp.arange(rows_here, dtype=jnp.int32)[None, :]).reshape(-1)
    key_pos = positions_of(block_order, token_rows, half_rows)

    queries3 = queries.reshape(rows_here, heads_here, width_qk)
    query_rows = me_ctx * rows_here + jnp.arange(rows_here, dtype=jnp.int32)
    query_pos = positions_of(block_order, query_rows, half_rows)

    row_count = piece.shape[0]
    packed = jnp.dot(piece[:, :LATENT], w_kv_up, preferred_element_type=jnp.float32)
    packed = packed.reshape(row_count, heads_here, width_kv)
    keys = packed[:, :, :HEAD_DIM]
    values = packed[:, :, HEAD_DIM:]
    rotary = piece[:, LATENT:]

    per_target = ctx_size // head_size
    if ctx_size > DIRECT_LIMIT:
        slot_of_block = jnp.arange(ctx_size, dtype=jnp.int32)
    else:
        slot_of_block = (me_ctx - jnp.arange(ctx_size, dtype=jnp.int32)) % ctx_size
    relative_targets = jnp.arange(head_size, dtype=jnp.int32) ^ me_head
    wanted_blocks = (relative_targets[:, None] * per_target + jnp.arange(per_target, dtype=jnp.int32)[None, :]).reshape(-1)
    wanted_slots = slot_of_block[wanted_blocks]

    query_nope = queries3[:, :, :HEAD_DIM].astype(jnp.float32)
    query_rope = queries3[:, :, HEAD_DIM:]
    scores = jnp.einsum("qhd,khd->qhk", query_nope, keys, precision=highest_p)
    scores = scores + jnp.einsum("qhd,kd->qhk", query_rope, rotary, preferred_element_type=jnp.float32)
    scores = scores * scaling
    visible = (key_pos[None, :] <= query_pos[:, None])[:, None, :]
    scores = jnp.where(visible, scores, NEGATIVE)
    highest = jnp.max(scores, axis=2, keepdims=True)
    weights = jnp.where(visible, jnp.exp(scores - highest), 0.0)
    totals = jnp.sum(weights, axis=2, keepdims=True)
    widened = lax.optimization_barrier(weights.astype(jnp.bfloat16)).astype(jnp.float32)
    mixed = jnp.einsum("qhk,khd->qhd", widened, values, precision=highest_p)
    outputs = (mixed / totals).astype(jnp.bfloat16).reshape(rows_here, heads_here * V_DIM)

    chunk_rows = rows_here // chunks
    results = []
    previous = None
    for chunk in range(chunks):
        part = outputs[chunk * chunk_rows:(chunk + 1) * chunk_rows]
        if previous is not None:
            part, previous = lax.optimization_barrier((part, previous))
        out_blocks, _ = gather_ctx(part, ctx_size)
        previous = out_blocks
        ordered = jnp.take(out_blocks, wanted_slots, axis=0)
        ordered = ordered.reshape(head_size, per_target * chunk_rows, heads_here * V_DIM)
        partials = jnp.einsum("trf,fc->trc", ordered, w_out, preferred_element_type=jnp.float32)
        total = reduce_scatter_head(partials, head_size)
        results.append(total.reshape(per_target, chunk_rows, -1))
    joined = jnp.stack(results, axis=1).reshape(per_target * rows_here, -1)
    return joined.astype(jnp.bfloat16)


def solution(mesh):
    placed = (
        P(("grp", "ctx"), "head"),
        P(("grp", "ctx"), None),
        P(None, "head"),
        P("head", "ctx"),
        P("grp"),
    )
    body = lambda *args: on_device(*args, ctx_size=mesh.shape["ctx"], head_size=mesh.shape["head"], chunks=CHUNKS)
    return jax.shard_map(
        body, mesh=mesh, in_specs=placed, out_specs=P(("grp", "head"), "ctx"), check_vma=False
    )
```

```python
import math

import jax
import jax.numpy as jnp
from jax import lax
from jax.experimental import pallas as pl
from jax.experimental.pallas import tpu as pltpu
from jax.sharding import PartitionSpec as P

LATENT = 256
ROPE = 64
HEAD_DIM = 64
V_DIM = 64

NEGATIVE = -1e30
DIRECT_LIMIT = 8


def positions_of(block_order, global_rows, half_rows):
    block_index = global_rows // half_rows
    matches = block_index[:, None] == jnp.arange(block_order.shape[0], dtype=jnp.int32)[None, :]
    picked = jnp.sum(jnp.where(matches, block_order[None, :], 0), axis=1)
    return picked * half_rows + global_rows % half_rows


def gather_ctx(x, ctx_size):
    me = lax.axis_index("ctx")
    if ctx_size > DIRECT_LIMIT:
        whole = lax.all_gather(x, "ctx", axis=0, tiled=False)
        return whole, jnp.arange(ctx_size, dtype=jnp.int32)
    pieces = [x]
    for shift in range(1, ctx_size):
        pairs = [(i, (i + shift) % ctx_size) for i in range(ctx_size)]
        pieces.append(lax.ppermute(x, "ctx", pairs))
    sources = (me - jnp.arange(ctx_size, dtype=jnp.int32)) % ctx_size
    return jnp.stack(pieces), sources


def project_kernel(x_ref, w_ref, o_ref):
    o_ref[...] = jnp.dot(x_ref[...], w_ref[...], preferred_element_type=jnp.float32)


def project(x, w):
    whole = pl.BlockSpec(memory_space=pltpu.VMEM)
    return pl.pallas_call(
        project_kernel,
        out_shape=jax.ShapeDtypeStruct((x.shape[0], w.shape[1]), jnp.float32),
        in_specs=[whole, whole],
        out_specs=whole,
    )(x, w)


def reduce_scatter_head(relative, head_size):
    acc = relative
    bit = 1
    while bit < head_size:
        pairs = [(i, i ^ bit) for i in range(head_size)]
        grouped = acc.reshape((acc.shape[0] // 2, 2) + acc.shape[1:])
        kept = grouped[:, 0]
        sent = grouped[:, 1].astype(jnp.bfloat16)
        got = lax.ppermute(sent, "head", pairs)
        acc = kept + got.astype(jnp.float32)
        bit *= 2
    return acc[0]


def on_device(queries, latents, w_kv_up, w_out, block_order, *, ctx_size, head_size):
    rows_here = queries.shape[0]
    half_rows = rows_here // 2
    width_qk = HEAD_DIM + ROPE
    width_kv = HEAD_DIM + V_DIM
    heads_here = w_kv_up.shape[1] // width_kv
    scaling = 1.0 / math.sqrt(width_qk)
    highest_p = lax.Precision.HIGHEST
    me_ctx = lax.axis_index("ctx")
    me_head = lax.axis_index("head")

    blocks, sources = gather_ctx(latents, ctx_size)
    piece = blocks.reshape(ctx_size * rows_here, latents.shape[1])
    token_rows = (sources[:, None] * rows_here + jnp.arange(rows_here, dtype=jnp.int32)[None, :]).reshape(-1)

    queries3 = queries.reshape(rows_here, heads_here, width_qk)
    query_nope = queries3[:, :, :HEAD_DIM].astype(jnp.float32)
    query_rope = queries3[:, :, HEAD_DIM:]
    query_rows = me_ctx * rows_here + jnp.arange(rows_here, dtype=jnp.int32)
    query_pos = positions_of(block_order, query_rows, half_rows)

    row_count = piece.shape[0]
    packed = jnp.dot(piece[:, :LATENT], w_kv_up, preferred_element_type=jnp.float32)
    packed = packed.reshape(row_count, heads_here, width_kv)
    scores = jnp.einsum("qhd,khd->qhk", query_nope, packed[:, :, :HEAD_DIM], precision=highest_p)
    scores = scores + jnp.einsum(
        "qhd,kd->qhk", query_rope, piece[:, LATENT:], preferred_element_type=jnp.float32
    )
    scores = scores * scaling
    visible = (positions_of(block_order, token_rows, half_rows)[None, :] <= query_pos[:, None])[:, None, :]
    scores = jnp.where(visible, scores, NEGATIVE)
    highest = jnp.max(scores, axis=2, keepdims=True)
    weights = jnp.where(visible, jnp.exp(scores - highest), 0.0)
    totals = jnp.sum(weights, axis=2, keepdims=True)
    widened = lax.optimization_barrier(weights.astype(jnp.bfloat16)).astype(jnp.float32)
    mixed = jnp.einsum("qhk,khd->qhd", widened, packed[:, :, HEAD_DIM:], precision=highest_p)
    outputs = (mixed / totals).astype(jnp.bfloat16).reshape(rows_here, heads_here * V_DIM)

    out_blocks, out_sources = gather_ctx(outputs, ctx_size)
    per_target = ctx_size // head_size
    if ctx_size > DIRECT_LIMIT:
        slot_of_block = jnp.arange(ctx_size, dtype=jnp.int32)
    else:
        slot_of_block = (me_ctx - jnp.arange(ctx_size, dtype=jnp.int32)) % ctx_size
    relative_targets = jnp.arange(head_size, dtype=jnp.int32) ^ me_head
    wanted_blocks = (relative_targets[:, None] * per_target + jnp.arange(per_target, dtype=jnp.int32)[None, :]).reshape(-1)
    ordered = jnp.take(out_blocks, slot_of_block[wanted_blocks], axis=0)
    ordered = ordered.reshape(head_size, per_target * rows_here, heads_here * V_DIM)
    flat = ordered.reshape(head_size * per_target * rows_here, heads_here * V_DIM)
    partials = project(flat, w_out).reshape(head_size, per_target * rows_here, -1)
    total = reduce_scatter_head(partials, head_size)
    return total.astype(jnp.bfloat16)


def solution(mesh):
    placed = (
        P(("grp", "ctx"), "head"),
        P(("grp", "ctx"), None),
        P(None, "head"),
        P("head", "ctx"),
        P("grp"),
    )
    body = lambda *args: on_device(*args, ctx_size=mesh.shape["ctx"], head_size=mesh.shape["head"])
    return jax.shard_map(
        body, mesh=mesh, in_specs=placed, out_specs=P(("grp", "head"), "ctx"), check_vma=False
    )
```

```python
import math

import jax
import jax.numpy as jnp
from jax import lax
from jax.sharding import PartitionSpec as P

LATENT = 256
ROPE = 64
HEAD_DIM = 64
V_DIM = 64

NEGATIVE = -1e30
DIRECT_LIMIT = 8


def positions_of(block_order, global_rows, half_rows):
    block_index = global_rows // half_rows
    matches = block_index[:, None] == jnp.arange(block_order.shape[0], dtype=jnp.int32)[None, :]
    picked = jnp.sum(jnp.where(matches, block_order[None, :], 0), axis=1)
    return picked * half_rows + global_rows % half_rows


def gather_ctx(x, ctx_size):
    me = lax.axis_index("ctx")
    if ctx_size > DIRECT_LIMIT:
        whole = lax.all_gather(x, "ctx", axis=0, tiled=False)
        return whole, jnp.arange(ctx_size, dtype=jnp.int32)
    copies = jnp.broadcast_to(x[None], (ctx_size,) + x.shape)
    whole = lax.all_to_all(copies, "ctx", 0, 0, tiled=False)
    return whole, jnp.arange(ctx_size, dtype=jnp.int32)


def reduce_scatter_head(relative, head_size):
    acc = relative
    bit = 1
    while bit < head_size:
        pairs = [(i, i ^ bit) for i in range(head_size)]
        grouped = acc.reshape((acc.shape[0] // 2, 2) + acc.shape[1:])
        kept = grouped[:, 0]
        sent = grouped[:, 1].astype(jnp.bfloat16)
        got = lax.ppermute(sent, "head", pairs)
        acc = kept + got.astype(jnp.float32)
        bit *= 2
    return acc[0]


def on_device(queries, latents, w_kv_up, w_out, block_order, *, ctx_size, head_size):
    rows_here = queries.shape[0]
    half_rows = rows_here // 2
    width_qk = HEAD_DIM + ROPE
    width_kv = HEAD_DIM + V_DIM
    heads_here = w_kv_up.shape[1] // width_kv
    scaling = 1.0 / math.sqrt(width_qk)
    highest_p = lax.Precision.HIGHEST
    me_ctx = lax.axis_index("ctx")
    me_head = lax.axis_index("head")

    blocks, sources = gather_ctx(latents, ctx_size)
    piece = blocks.reshape(ctx_size * rows_here, latents.shape[1])
    token_rows = (sources[:, None] * rows_here + jnp.arange(rows_here, dtype=jnp.int32)[None, :]).reshape(-1)

    queries3 = queries.reshape(rows_here, heads_here, width_qk)
    query_nope = queries3[:, :, :HEAD_DIM].astype(jnp.float32)
    query_rope = queries3[:, :, HEAD_DIM:]
    query_rows = me_ctx * rows_here + jnp.arange(rows_here, dtype=jnp.int32)
    query_pos = positions_of(block_order, query_rows, half_rows)

    row_count = piece.shape[0]
    packed = jnp.dot(piece[:, :LATENT], w_kv_up, preferred_element_type=jnp.float32)
    packed = packed.reshape(row_count, heads_here, width_kv)
    scores = jnp.einsum("qhd,khd->qhk", query_nope, packed[:, :, :HEAD_DIM], precision=highest_p)
    scores = scores + jnp.einsum(
        "qhd,kd->qhk", query_rope, piece[:, LATENT:], preferred_element_type=jnp.float32
    )
    scores = scores * scaling
    visible = (positions_of(block_order, token_rows, half_rows)[None, :] <= query_pos[:, None])[:, None, :]
    scores = jnp.where(visible, scores, NEGATIVE)
    highest = jnp.max(scores, axis=2, keepdims=True)
    weights = jnp.where(visible, jnp.exp(scores - highest), 0.0)
    totals = jnp.sum(weights, axis=2, keepdims=True)
    widened = lax.optimization_barrier(weights.astype(jnp.bfloat16)).astype(jnp.float32)
    mixed = jnp.einsum("qhk,khd->qhd", widened, packed[:, :, HEAD_DIM:], precision=highest_p)
    outputs = (mixed / totals).astype(jnp.bfloat16).reshape(rows_here, heads_here * V_DIM)

    out_blocks, out_sources = gather_ctx(outputs, ctx_size)
    per_target = ctx_size // head_size
    slot_of_block = jnp.arange(ctx_size, dtype=jnp.int32)
    relative_targets = jnp.arange(head_size, dtype=jnp.int32) ^ me_head
    wanted_blocks = (relative_targets[:, None] * per_target + jnp.arange(per_target, dtype=jnp.int32)[None, :]).reshape(-1)
    ordered = jnp.take(out_blocks, slot_of_block[wanted_blocks], axis=0)
    ordered = ordered.reshape(head_size, per_target * rows_here, heads_here * V_DIM)
    partials = jnp.einsum("trf,fc->trc", ordered, w_out, preferred_element_type=jnp.float32)
    total = reduce_scatter_head(partials, head_size)
    return total.astype(jnp.bfloat16)


def solution(mesh):
    placed = (
        P(("grp", "ctx"), "head"),
        P(("grp", "ctx"), None),
        P(None, "head"),
        P("head", "ctx"),
        P("grp"),
    )
    body = lambda *args: on_device(*args, ctx_size=mesh.shape["ctx"], head_size=mesh.shape["head"])
    return jax.shard_map(
        body, mesh=mesh, in_specs=placed, out_specs=P(("grp", "head"), "ctx"), check_vma=False
    )
```

```python
import math

import jax
import jax.numpy as jnp
from jax import lax
from jax.experimental import pallas as pl
from jax.experimental.pallas import tpu as pltpu
from jax.sharding import PartitionSpec as P

LATENT = 256
ROPE = 64
HEAD_DIM = 64
V_DIM = 64

NEGATIVE = -1e30
DIRECT_LIMIT = 8
STAGE_WIDTH = 256


def positions_of(block_order, global_rows, half_rows):
    block_index = global_rows // half_rows
    matches = block_index[:, None] == jnp.arange(block_order.shape[0], dtype=jnp.int32)[None, :]
    picked = jnp.sum(jnp.where(matches, block_order[None, :], 0), axis=1)
    return picked * half_rows + global_rows % half_rows


def gather_ctx(x, ctx_size):
    me = lax.axis_index("ctx")
    if ctx_size > DIRECT_LIMIT:
        whole = lax.all_gather(x, "ctx", axis=0, tiled=False)
        return whole, jnp.arange(ctx_size, dtype=jnp.int32)
    pieces = [x]
    for shift in range(1, ctx_size):
        pairs = [(i, (i + shift) % ctx_size) for i in range(ctx_size)]
        pieces.append(lax.ppermute(x, "ctx", pairs))
    sources = (me - jnp.arange(ctx_size, dtype=jnp.int32)) % ctx_size
    return jnp.stack(pieces), sources


def stage_kernel(w_ref, o_ref):
    o_ref[...] = w_ref[...]


def stage_columns(w):
    width = STAGE_WIDTH if w.shape[1] % STAGE_WIDTH == 0 else w.shape[1]
    blocks = []
    for k in range(w.shape[1] // width):
        blocks.append(pl.pallas_call(
            stage_kernel,
            out_shape=pltpu.VMEM((w.shape[0], width), w.dtype),
            grid=(1,),
            in_specs=[pl.BlockSpec((w.shape[0], width), lambda i, k=k: (0, k))],
            out_specs=pl.BlockSpec((w.shape[0], width), lambda i: (0, 0)),
        )(w))
    return blocks


def reduce_scatter_head(relative, head_size):
    acc = relative
    bit = 1
    while bit < head_size:
        pairs = [(i, i ^ bit) for i in range(head_size)]
        grouped = acc.reshape((acc.shape[0] // 2, 2) + acc.shape[1:])
        kept = grouped[:, 0]
        sent = grouped[:, 1].astype(jnp.bfloat16)
        got = lax.ppermute(sent, "head", pairs)
        acc = kept + got.astype(jnp.float32)
        bit *= 2
    return acc[0]


def on_device(queries, latents, w_kv_up, w_out, block_order, *, ctx_size, head_size):
    rows_here = queries.shape[0]
    half_rows = rows_here // 2
    width_qk = HEAD_DIM + ROPE
    width_kv = HEAD_DIM + V_DIM
    heads_here = w_kv_up.shape[1] // width_kv
    scaling = 1.0 / math.sqrt(width_qk)
    highest_p = lax.Precision.HIGHEST
    me_ctx = lax.axis_index("ctx")
    me_head = lax.axis_index("head")

    staged = stage_columns(w_out)
    blocks, sources = gather_ctx(latents, ctx_size)
    piece = blocks.reshape(ctx_size * rows_here, latents.shape[1])
    token_rows = (sources[:, None] * rows_here + jnp.arange(rows_here, dtype=jnp.int32)[None, :]).reshape(-1)

    queries3 = queries.reshape(rows_here, heads_here, width_qk)
    query_nope = queries3[:, :, :HEAD_DIM].astype(jnp.float32)
    query_rope = queries3[:, :, HEAD_DIM:]
    query_rows = me_ctx * rows_here + jnp.arange(rows_here, dtype=jnp.int32)
    query_pos = positions_of(block_order, query_rows, half_rows)

    row_count = piece.shape[0]
    packed = jnp.dot(piece[:, :LATENT], w_kv_up, preferred_element_type=jnp.float32)
    packed = packed.reshape(row_count, heads_here, width_kv)
    scores = jnp.einsum("qhd,khd->qhk", query_nope, packed[:, :, :HEAD_DIM], precision=highest_p)
    scores = scores + jnp.einsum(
        "qhd,kd->qhk", query_rope, piece[:, LATENT:], preferred_element_type=jnp.float32
    )
    scores = scores * scaling
    visible = (positions_of(block_order, token_rows, half_rows)[None, :] <= query_pos[:, None])[:, None, :]
    scores = jnp.where(visible, scores, NEGATIVE)
    highest = jnp.max(scores, axis=2, keepdims=True)
    weights = jnp.where(visible, jnp.exp(scores - highest), 0.0)
    totals = jnp.sum(weights, axis=2, keepdims=True)
    widened = lax.optimization_barrier(weights.astype(jnp.bfloat16)).astype(jnp.float32)
    mixed = jnp.einsum("qhk,khd->qhd", widened, packed[:, :, HEAD_DIM:], precision=highest_p)
    outputs = (mixed / totals).astype(jnp.bfloat16).reshape(rows_here, heads_here * V_DIM)

    out_blocks, out_sources = gather_ctx(outputs, ctx_size)
    per_target = ctx_size // head_size
    if ctx_size > DIRECT_LIMIT:
        slot_of_block = jnp.arange(ctx_size, dtype=jnp.int32)
    else:
        slot_of_block = (me_ctx - jnp.arange(ctx_size, dtype=jnp.int32)) % ctx_size
    relative_targets = jnp.arange(head_size, dtype=jnp.int32) ^ me_head
    wanted_blocks = (relative_targets[:, None] * per_target + jnp.arange(per_target, dtype=jnp.int32)[None, :]).reshape(-1)
    ordered = jnp.take(out_blocks, slot_of_block[wanted_blocks], axis=0)
    ordered = ordered.reshape(head_size, per_target * rows_here, heads_here * V_DIM)
    partials = jnp.concatenate(
        [jnp.einsum("trf,fc->trc", ordered, block, preferred_element_type=jnp.float32) for block in staged],
        axis=2,
    )
    total = reduce_scatter_head(partials, head_size)
    return total.astype(jnp.bfloat16)


def solution(mesh):
    placed = (
        P(("grp", "ctx"), "head"),
        P(("grp", "ctx"), None),
        P(None, "head"),
        P("head", "ctx"),
        P("grp"),
    )
    body = lambda *args: on_device(*args, ctx_size=mesh.shape["ctx"], head_size=mesh.shape["head"])
    return jax.shard_map(
        body, mesh=mesh, in_specs=placed, out_specs=P(("grp", "head"), "ctx"), check_vma=False
    )
```

```python
import math

import jax
import jax.numpy as jnp
from jax import lax
from jax.sharding import PartitionSpec as P

LATENT = 256
ROPE = 64
HEAD_DIM = 64
V_DIM = 64

NEGATIVE = -1e30
DIRECT_LIMIT = 8


def positions_of(block_order, global_rows, half_rows):
    block_index = global_rows // half_rows
    matches = block_index[:, None] == jnp.arange(block_order.shape[0], dtype=jnp.int32)[None, :]
    picked = jnp.sum(jnp.where(matches, block_order[None, :], 0), axis=1)
    return picked * half_rows + global_rows % half_rows


def gather_ctx(x, ctx_size):
    me = lax.axis_index("ctx")
    if ctx_size > DIRECT_LIMIT:
        whole = lax.all_gather(x, "ctx", axis=0, tiled=False)
        return whole, jnp.arange(ctx_size, dtype=jnp.int32)
    pieces = [x]
    for shift in range(1, ctx_size):
        pairs = [(i, (i + shift) % ctx_size) for i in range(ctx_size)]
        pieces.append(lax.ppermute(x, "ctx", pairs))
    sources = (me - jnp.arange(ctx_size, dtype=jnp.int32)) % ctx_size
    return jnp.stack(pieces), sources


def reduce_scatter_head(slabs, head_size):
    bit = 1
    while bit < head_size:
        pairs = [(i, i ^ bit) for i in range(head_size)]
        kept = slabs[0::2]
        sent = jnp.stack([slab.astype(jnp.bfloat16) for slab in slabs[1::2]])
        got = lax.ppermute(sent, "head", pairs)
        slabs = [slab + got[i].astype(jnp.float32) for i, slab in enumerate(kept)]
        bit *= 2
    return slabs[0]


def on_device(queries, latents, w_kv_up, w_out, block_order, *, ctx_size, head_size):
    rows_here = queries.shape[0]
    half_rows = rows_here // 2
    width_qk = HEAD_DIM + ROPE
    width_kv = HEAD_DIM + V_DIM
    heads_here = w_kv_up.shape[1] // width_kv
    scaling = 1.0 / math.sqrt(width_qk)
    highest_p = lax.Precision.HIGHEST
    me_ctx = lax.axis_index("ctx")
    me_head = lax.axis_index("head")

    blocks, sources = gather_ctx(latents, ctx_size)
    piece = blocks.reshape(ctx_size * rows_here, latents.shape[1])
    token_rows = (sources[:, None] * rows_here + jnp.arange(rows_here, dtype=jnp.int32)[None, :]).reshape(-1)

    queries3 = queries.reshape(rows_here, heads_here, width_qk)
    query_nope = queries3[:, :, :HEAD_DIM].astype(jnp.float32)
    query_rope = queries3[:, :, HEAD_DIM:]
    query_rows = me_ctx * rows_here + jnp.arange(rows_here, dtype=jnp.int32)
    query_pos = positions_of(block_order, query_rows, half_rows)

    row_count = piece.shape[0]
    packed = jnp.dot(piece[:, :LATENT], w_kv_up, preferred_element_type=jnp.float32)
    packed = packed.reshape(row_count, heads_here, width_kv)
    scores = jnp.einsum("qhd,khd->qhk", query_nope, packed[:, :, :HEAD_DIM], precision=highest_p)
    scores = scores + jnp.einsum(
        "qhd,kd->qhk", query_rope, piece[:, LATENT:], preferred_element_type=jnp.float32
    )
    scores = scores * scaling
    visible = (positions_of(block_order, token_rows, half_rows)[None, :] <= query_pos[:, None])[:, None, :]
    scores = jnp.where(visible, scores, NEGATIVE)
    highest = jnp.max(scores, axis=2, keepdims=True)
    weights = jnp.where(visible, jnp.exp(scores - highest), 0.0)
    totals = jnp.sum(weights, axis=2, keepdims=True)
    widened = lax.optimization_barrier(weights.astype(jnp.bfloat16)).astype(jnp.float32)
    mixed = jnp.einsum("qhk,khd->qhd", widened, packed[:, :, HEAD_DIM:], precision=highest_p)
    outputs = (mixed / totals).astype(jnp.bfloat16).reshape(rows_here, heads_here * V_DIM)

    per_target = ctx_size // head_size
    relative_targets = jnp.arange(head_size, dtype=jnp.int32) ^ me_head
    if ctx_size == head_size and ctx_size <= DIRECT_LIMIT:
        own = jnp.dot(outputs, w_out, preferred_element_type=jnp.float32)
        out_blocks, _ = gather_ctx(outputs, ctx_size)
        others = jnp.einsum("srf,fc->src", out_blocks[1:], w_out, preferred_element_type=jnp.float32)
        products = jnp.concatenate([own[None], others], axis=0)
        shift_of = (me_ctx - relative_targets) % ctx_size
        slabs = [lax.dynamic_index_in_dim(products, shift_of[u], 0, keepdims=False) for u in range(head_size)]
    else:
        out_blocks, _ = gather_ctx(outputs, ctx_size)
        if ctx_size > DIRECT_LIMIT:
            slot_of_block = jnp.arange(ctx_size, dtype=jnp.int32)
        else:
            slot_of_block = (me_ctx - jnp.arange(ctx_size, dtype=jnp.int32)) % ctx_size
        wanted_blocks = (relative_targets[:, None] * per_target + jnp.arange(per_target, dtype=jnp.int32)[None, :]).reshape(-1)
        ordered = jnp.take(out_blocks, slot_of_block[wanted_blocks], axis=0)
        ordered = ordered.reshape(head_size, per_target * rows_here, heads_here * V_DIM)
        products = jnp.einsum("trf,fc->trc", ordered, w_out, preferred_element_type=jnp.float32)
        slabs = [products[u] for u in range(head_size)]
    total = reduce_scatter_head(slabs, head_size)
    return total.astype(jnp.bfloat16)


def solution(mesh):
    placed = (
        P(("grp", "ctx"), "head"),
        P(("grp", "ctx"), None),
        P(None, "head"),
        P("head", "ctx"),
        P("grp"),
    )
    body = lambda *args: on_device(*args, ctx_size=mesh.shape["ctx"], head_size=mesh.shape["head"])
    return jax.shard_map(
        body, mesh=mesh, in_specs=placed, out_specs=P(("grp", "head"), "ctx"), check_vma=False
    )
```

```python
import math

import jax
import jax.numpy as jnp
from jax import lax
from jax.sharding import PartitionSpec as P

LATENT = 256
ROPE = 64
HEAD_DIM = 64
V_DIM = 64

NEGATIVE = -1e30
DIRECT_LIMIT = 8


def positions_of(block_order, global_rows, half_rows):
    block_index = global_rows // half_rows
    matches = block_index[:, None] == jnp.arange(block_order.shape[0], dtype=jnp.int32)[None, :]
    picked = jnp.sum(jnp.where(matches, block_order[None, :], 0), axis=1)
    return picked * half_rows + global_rows % half_rows


def gather_ctx(x, ctx_size):
    me = lax.axis_index("ctx")
    if ctx_size > DIRECT_LIMIT:
        whole = lax.all_gather(x, "ctx", axis=0, tiled=False)
        return whole, jnp.arange(ctx_size, dtype=jnp.int32)
    pieces = [x]
    for shift in range(1, ctx_size):
        pairs = [(i, (i + shift) % ctx_size) for i in range(ctx_size)]
        pieces.append(lax.ppermute(x, "ctx", pairs))
    sources = (me - jnp.arange(ctx_size, dtype=jnp.int32)) % ctx_size
    return jnp.stack(pieces), sources


def reduce_scatter_head(slabs, head_size):
    bit = 1
    while bit < head_size:
        pairs = [(i, i ^ bit) for i in range(head_size)]
        kept = slabs[0::2]
        sent = jnp.stack([slab.astype(jnp.bfloat16) for slab in slabs[1::2]])
        got = lax.ppermute(sent, "head", pairs)
        slabs = [slab + got[i].astype(jnp.float32) for i, slab in enumerate(kept)]
        bit *= 2
    return slabs[0]


def on_device(queries, latents, w_kv_up, w_out, block_order, *, ctx_size, head_size):
    rows_here = queries.shape[0]
    half_rows = rows_here // 2
    width_qk = HEAD_DIM + ROPE
    width_kv = HEAD_DIM + V_DIM
    heads_here = w_kv_up.shape[1] // width_kv
    scaling = 1.0 / math.sqrt(width_qk)
    highest_p = lax.Precision.HIGHEST
    me_ctx = lax.axis_index("ctx")
    me_head = lax.axis_index("head")

    blocks, sources = gather_ctx(latents, ctx_size)
    piece = blocks.reshape(ctx_size * rows_here, latents.shape[1])
    token_rows = (sources[:, None] * rows_here + jnp.arange(rows_here, dtype=jnp.int32)[None, :]).reshape(-1)

    queries3 = queries.reshape(rows_here, heads_here, width_qk)
    query_nope = queries3[:, :, :HEAD_DIM].astype(jnp.float32)
    query_rope = queries3[:, :, HEAD_DIM:]
    query_rows = me_ctx * rows_here + jnp.arange(rows_here, dtype=jnp.int32)
    query_pos = positions_of(block_order, query_rows, half_rows)

    row_count = piece.shape[0]
    packed = jnp.dot(piece[:, :LATENT], w_kv_up, preferred_element_type=jnp.float32)
    packed = packed.reshape(row_count, heads_here, width_kv)
    scores = jnp.einsum("qhd,khd->qhk", query_nope, packed[:, :, :HEAD_DIM], precision=highest_p)
    scores = scores + jnp.einsum(
        "qhd,kd->qhk", query_rope, piece[:, LATENT:], preferred_element_type=jnp.float32
    )
    scores = scores * scaling
    visible = (positions_of(block_order, token_rows, half_rows)[None, :] <= query_pos[:, None])[:, None, :]
    scores = jnp.where(visible, scores, NEGATIVE)
    highest = jnp.max(scores, axis=2, keepdims=True)
    weights = jnp.where(visible, jnp.exp(scores - highest), 0.0)
    totals = jnp.sum(weights, axis=2, keepdims=True)
    widened = lax.optimization_barrier(weights.astype(jnp.bfloat16)).astype(jnp.float32)
    mixed = jnp.einsum("qhk,khd->qhd", widened, packed[:, :, HEAD_DIM:], precision=highest_p)
    outputs = (mixed / totals).astype(jnp.bfloat16).reshape(rows_here, heads_here * V_DIM)

    per_target = ctx_size // head_size
    relative_targets = jnp.arange(head_size, dtype=jnp.int32) ^ me_head
    if ctx_size == head_size and ctx_size <= DIRECT_LIMIT:
        own = jnp.dot(outputs, w_out, preferred_element_type=jnp.float32)
        out_blocks, _ = gather_ctx(outputs, ctx_size)
        others = jnp.einsum("srf,fc->src", out_blocks[1:], w_out, preferred_element_type=jnp.float32)
        products = jnp.concatenate([own[None], others], axis=0)
        shift_of = (me_ctx - relative_targets) % ctx_size
        relative = jnp.take(products, shift_of, axis=0)
        slabs = [relative[u] for u in range(head_size)]
    else:
        out_blocks, _ = gather_ctx(outputs, ctx_size)
        if ctx_size > DIRECT_LIMIT:
            slot_of_block = jnp.arange(ctx_size, dtype=jnp.int32)
        else:
            slot_of_block = (me_ctx - jnp.arange(ctx_size, dtype=jnp.int32)) % ctx_size
        wanted_blocks = (relative_targets[:, None] * per_target + jnp.arange(per_target, dtype=jnp.int32)[None, :]).reshape(-1)
        ordered = jnp.take(out_blocks, slot_of_block[wanted_blocks], axis=0)
        ordered = ordered.reshape(head_size, per_target * rows_here, heads_here * V_DIM)
        products = jnp.einsum("trf,fc->trc", ordered, w_out, preferred_element_type=jnp.float32)
        slabs = [products[u] for u in range(head_size)]
    total = reduce_scatter_head(slabs, head_size)
    return total.astype(jnp.bfloat16)


def solution(mesh):
    placed = (
        P(("grp", "ctx"), "head"),
        P(("grp", "ctx"), None),
        P(None, "head"),
        P("head", "ctx"),
        P("grp"),
    )
    body = lambda *args: on_device(*args, ctx_size=mesh.shape["ctx"], head_size=mesh.shape["head"])
    return jax.shard_map(
        body, mesh=mesh, in_specs=placed, out_specs=P(("grp", "head"), "ctx"), check_vma=False
    )
```

```python
import math

import jax
import jax.numpy as jnp
from jax import lax
from jax.sharding import PartitionSpec as P

LATENT = 256
ROPE = 64
HEAD_DIM = 64
V_DIM = 64

NEGATIVE = -1e30
DIRECT_LIMIT = 8


def positions_of(block_order, global_rows, half_rows):
    block_index = global_rows // half_rows
    matches = block_index[:, None] == jnp.arange(block_order.shape[0], dtype=jnp.int32)[None, :]
    picked = jnp.sum(jnp.where(matches, block_order[None, :], 0), axis=1)
    return picked * half_rows + global_rows % half_rows


def gather_ctx(x, ctx_size):
    me = lax.axis_index("ctx")
    if ctx_size > DIRECT_LIMIT:
        whole = lax.all_gather(x, "ctx", axis=0, tiled=False)
        return whole, jnp.arange(ctx_size, dtype=jnp.int32)
    pieces = [x]
    for shift in range(1, ctx_size):
        pairs = [(i, (i + shift) % ctx_size) for i in range(ctx_size)]
        pieces.append(lax.ppermute(x, "ctx", pairs))
    sources = (me - jnp.arange(ctx_size, dtype=jnp.int32)) % ctx_size
    return jnp.stack(pieces), sources


def reduce_scatter_head(slabs, head_size):
    bit = 1
    while bit < head_size:
        pairs = [(i, i ^ bit) for i in range(head_size)]
        kept = slabs[0::2]
        sent = jnp.stack([slab.astype(jnp.bfloat16) for slab in slabs[1::2]])
        got = lax.ppermute(sent, "head", pairs)
        slabs = [slab + got[i].astype(jnp.float32) for i, slab in enumerate(kept)]
        bit *= 2
    return slabs[0]


def on_device(queries, latents, w_kv_up, w_out, block_order, *, ctx_size, head_size):
    rows_here = queries.shape[0]
    half_rows = rows_here // 2
    width_qk = HEAD_DIM + ROPE
    width_kv = HEAD_DIM + V_DIM
    heads_here = w_kv_up.shape[1] // width_kv
    scaling = 1.0 / math.sqrt(width_qk)
    highest_p = lax.Precision.HIGHEST
    me_ctx = lax.axis_index("ctx")
    me_head = lax.axis_index("head")

    blocks, sources = gather_ctx(latents, ctx_size)
    piece = blocks.reshape(ctx_size * rows_here, latents.shape[1])
    token_rows = (sources[:, None] * rows_here + jnp.arange(rows_here, dtype=jnp.int32)[None, :]).reshape(-1)

    queries3 = queries.reshape(rows_here, heads_here, width_qk)
    query_nope = queries3[:, :, :HEAD_DIM].astype(jnp.float32)
    query_rope = queries3[:, :, HEAD_DIM:]
    query_rows = me_ctx * rows_here + jnp.arange(rows_here, dtype=jnp.int32)
    query_pos = positions_of(block_order, query_rows, half_rows)

    row_count = piece.shape[0]
    packed = jnp.dot(piece[:, :LATENT], w_kv_up, preferred_element_type=jnp.float32)
    packed = packed.reshape(row_count, heads_here, width_kv)
    scores = jnp.einsum("qhd,khd->qhk", query_nope, packed[:, :, :HEAD_DIM], precision=highest_p)
    scores = scores + jnp.einsum(
        "qhd,kd->qhk", query_rope, piece[:, LATENT:], preferred_element_type=jnp.float32
    )
    scores = scores * scaling
    visible = (positions_of(block_order, token_rows, half_rows)[None, :] <= query_pos[:, None])[:, None, :]
    scores = jnp.where(visible, scores, NEGATIVE)
    highest = jnp.max(scores, axis=2, keepdims=True)
    weights = jnp.where(visible, jnp.exp(scores - highest), 0.0)
    totals = jnp.sum(weights, axis=2, keepdims=True)
    widened = lax.optimization_barrier(weights.astype(jnp.bfloat16)).astype(jnp.float32)
    mixed = jnp.einsum("qhk,khd->qhd", widened, packed[:, :, HEAD_DIM:], precision=highest_p)
    outputs = (mixed / totals).astype(jnp.bfloat16).reshape(rows_here, heads_here * V_DIM)

    per_target = ctx_size // head_size
    relative_targets = jnp.arange(head_size, dtype=jnp.int32) ^ me_head
    if ctx_size == head_size and ctx_size <= DIRECT_LIMIT:
        relative_of_shift = ((me_ctx - jnp.arange(ctx_size, dtype=jnp.int32)) % ctx_size) ^ me_head
        own = jnp.dot(outputs, w_out, preferred_element_type=jnp.float32)
        products = jnp.zeros((head_size,) + own.shape, jnp.float32)
        products = lax.dynamic_update_index_in_dim(products, own, relative_of_shift[0], 0)
        out_blocks, _ = gather_ctx(outputs, ctx_size)
        for shift in range(1, ctx_size):
            part = jnp.dot(out_blocks[shift], w_out, preferred_element_type=jnp.float32)
            products = lax.dynamic_update_index_in_dim(products, part, relative_of_shift[shift], 0)
        slabs = [products[u] for u in range(head_size)]
    else:
        out_blocks, _ = gather_ctx(outputs, ctx_size)
        if ctx_size > DIRECT_LIMIT:
            slot_of_block = jnp.arange(ctx_size, dtype=jnp.int32)
        else:
            slot_of_block = (me_ctx - jnp.arange(ctx_size, dtype=jnp.int32)) % ctx_size
        wanted_blocks = (relative_targets[:, None] * per_target + jnp.arange(per_target, dtype=jnp.int32)[None, :]).reshape(-1)
        ordered = jnp.take(out_blocks, slot_of_block[wanted_blocks], axis=0)
        ordered = ordered.reshape(head_size, per_target * rows_here, heads_here * V_DIM)
        products = jnp.einsum("trf,fc->trc", ordered, w_out, preferred_element_type=jnp.float32)
        slabs = [products[u] for u in range(head_size)]
    total = reduce_scatter_head(slabs, head_size)
    return total.astype(jnp.bfloat16)


def solution(mesh):
    placed = (
        P(("grp", "ctx"), "head"),
        P(("grp", "ctx"), None),
        P(None, "head"),
        P("head", "ctx"),
        P("grp"),
    )
    body = lambda *args: on_device(*args, ctx_size=mesh.shape["ctx"], head_size=mesh.shape["head"])
    return jax.shard_map(
        body, mesh=mesh, in_specs=placed, out_specs=P(("grp", "head"), "ctx"), check_vma=False
    )
```

```python
import math

import jax
import jax.numpy as jnp
from jax import lax
from jax.sharding import PartitionSpec as P

LATENT = 256
ROPE = 64
HEAD_DIM = 64
V_DIM = 64

NEGATIVE = -1e30
DIRECT_LIMIT = 8


def positions_of(block_order, global_rows, half_rows):
    block_index = global_rows // half_rows
    matches = block_index[:, None] == jnp.arange(block_order.shape[0], dtype=jnp.int32)[None, :]
    picked = jnp.sum(jnp.where(matches, block_order[None, :], 0), axis=1)
    return picked * half_rows + global_rows % half_rows


def gather_ctx(x, ctx_size):
    me = lax.axis_index("ctx")
    if ctx_size > DIRECT_LIMIT:
        whole = lax.all_gather(x, "ctx", axis=0, tiled=False)
        return whole, jnp.arange(ctx_size, dtype=jnp.int32)
    pieces = [x]
    for shift in range(1, ctx_size):
        pairs = [(i, (i + shift) % ctx_size) for i in range(ctx_size)]
        pieces.append(lax.ppermute(x, "ctx", pairs))
    sources = (me - jnp.arange(ctx_size, dtype=jnp.int32)) % ctx_size
    return jnp.stack(pieces), sources


def reduce_scatter_head(relative, head_size):
    acc = relative
    bit = 1
    while bit < head_size:
        pairs = [(i, i ^ bit) for i in range(head_size)]
        grouped = acc.reshape((acc.shape[0] // 2, 2) + acc.shape[1:])
        kept = grouped[:, 0]
        sent = grouped[:, 1].astype(jnp.bfloat16)
        got = lax.ppermute(sent, "head", pairs)
        acc = kept + got.astype(jnp.float32)
        bit *= 2
    return acc[0]


def on_device(queries, latents, w_kv_up, w_out, block_order, *, ctx_size, head_size):
    rows_here = queries.shape[0]
    half_rows = rows_here // 2
    width_qk = HEAD_DIM + ROPE
    width_kv = HEAD_DIM + V_DIM
    heads_here = w_kv_up.shape[1] // width_kv
    scaling = 1.0 / math.sqrt(width_qk)
    highest_p = lax.Precision.HIGHEST
    me_ctx = lax.axis_index("ctx")
    me_head = lax.axis_index("head")

    blocks, sources = gather_ctx(latents, ctx_size)

    queries3 = queries.reshape(rows_here, heads_here, width_qk)
    query_nope = queries3[:, :, :HEAD_DIM].astype(jnp.float32)
    query_rope = queries3[:, :, HEAD_DIM:]
    query_rows = me_ctx * rows_here + jnp.arange(rows_here, dtype=jnp.int32)
    query_pos = positions_of(block_order, query_rows, half_rows)

    piece_scores = []
    piece_values = []
    piece_visible = []
    for slot in range(blocks.shape[0]):
        piece = blocks[slot]
        token_rows = sources[slot] * rows_here + jnp.arange(rows_here, dtype=jnp.int32)
        packed = jnp.dot(piece[:, :LATENT], w_kv_up, preferred_element_type=jnp.float32)
        packed = packed.reshape(rows_here, heads_here, width_kv)
        scores = jnp.einsum("qhd,khd->qhk", query_nope, packed[:, :, :HEAD_DIM], precision=highest_p)
        scores = scores + jnp.einsum(
            "qhd,kd->qhk", query_rope, piece[:, LATENT:], preferred_element_type=jnp.float32
        )
        scores = scores * scaling
        visible = (positions_of(block_order, token_rows, half_rows)[None, :] <= query_pos[:, None])[:, None, :]
        piece_scores.append(jnp.where(visible, scores, NEGATIVE))
        piece_values.append(packed[:, :, HEAD_DIM:])
        piece_visible.append(visible)
    highest = piece_scores[0].max(axis=2, keepdims=True)
    for scores in piece_scores[1:]:
        highest = jnp.maximum(highest, scores.max(axis=2, keepdims=True))
    totals = None
    mixed = None
    for scores, values, visible in zip(piece_scores, piece_values, piece_visible):
        weights = jnp.where(visible, jnp.exp(scores - highest), 0.0)
        part_total = jnp.sum(weights, axis=2, keepdims=True)
        widened = lax.optimization_barrier(weights.astype(jnp.bfloat16)).astype(jnp.float32)
        part_mixed = jnp.einsum("qhk,khd->qhd", widened, values, precision=highest_p)
        totals = part_total if totals is None else totals + part_total
        mixed = part_mixed if mixed is None else mixed + part_mixed
    outputs = (mixed / totals).astype(jnp.bfloat16).reshape(rows_here, heads_here * V_DIM)

    out_blocks, out_sources = gather_ctx(outputs, ctx_size)
    per_target = ctx_size // head_size
    if ctx_size > DIRECT_LIMIT:
        slot_of_block = jnp.arange(ctx_size, dtype=jnp.int32)
    else:
        slot_of_block = (me_ctx - jnp.arange(ctx_size, dtype=jnp.int32)) % ctx_size
    relative_targets = jnp.arange(head_size, dtype=jnp.int32) ^ me_head
    wanted_blocks = (relative_targets[:, None] * per_target + jnp.arange(per_target, dtype=jnp.int32)[None, :]).reshape(-1)
    ordered = jnp.take(out_blocks, slot_of_block[wanted_blocks], axis=0)
    ordered = ordered.reshape(head_size, per_target * rows_here, heads_here * V_DIM)
    partials = jnp.einsum("trf,fc->trc", ordered, w_out, preferred_element_type=jnp.float32)
    total = reduce_scatter_head(partials, head_size)
    return total.astype(jnp.bfloat16)


def solution(mesh):
    placed = (
        P(("grp", "ctx"), "head"),
        P(("grp", "ctx"), None),
        P(None, "head"),
        P("head", "ctx"),
        P("grp"),
    )
    body = lambda *args: on_device(*args, ctx_size=mesh.shape["ctx"], head_size=mesh.shape["head"])
    return jax.shard_map(
        body, mesh=mesh, in_specs=placed, out_specs=P(("grp", "head"), "ctx"), check_vma=False
    )
```

```python
import math

import jax
import jax.numpy as jnp
from jax import lax
from jax.sharding import PartitionSpec as P

LATENT = 256
ROPE = 64
HEAD_DIM = 64
V_DIM = 64

NEGATIVE = -1e30
DIRECT_LIMIT = 8


def positions_of(block_order, global_rows, half_rows):
    block_index = global_rows // half_rows
    matches = block_index[:, None] == jnp.arange(block_order.shape[0], dtype=jnp.int32)[None, :]
    picked = jnp.sum(jnp.where(matches, block_order[None, :], 0), axis=1)
    return picked * half_rows + global_rows % half_rows


def gather_ctx(x, ctx_size):
    me = lax.axis_index("ctx")
    if ctx_size > DIRECT_LIMIT:
        whole = lax.all_gather(x, "ctx", axis=0, tiled=False)
        return whole, jnp.arange(ctx_size, dtype=jnp.int32)
    pieces = [x]
    for step in range(1, ctx_size):
        pairs = [(partner_of(i, step, ctx_size), i) for i in range(ctx_size)]
        pieces.append(lax.ppermute(x, "ctx", pairs))
    sources = jnp.stack([partner_of(me, step, ctx_size) for step in range(ctx_size)]).astype(jnp.int32)
    return jnp.stack(pieces), sources


def partner_of(i, step, size):
    if size & (size - 1) == 0:
        return i ^ step
    return (i - step) % size


def reduce_scatter_head(relative, head_size):
    acc = relative
    bit = 1
    while bit < head_size:
        pairs = [(i, i ^ bit) for i in range(head_size)]
        grouped = acc.reshape((acc.shape[0] // 2, 2) + acc.shape[1:])
        kept = grouped[:, 0]
        sent = grouped[:, 1].astype(jnp.bfloat16)
        got = lax.ppermute(sent, "head", pairs)
        acc = kept + got.astype(jnp.float32)
        bit *= 2
    return acc[0]


def on_device(queries, latents, w_kv_up, w_out, block_order, *, ctx_size, head_size):
    rows_here = queries.shape[0]
    half_rows = rows_here // 2
    width_qk = HEAD_DIM + ROPE
    width_kv = HEAD_DIM + V_DIM
    heads_here = w_kv_up.shape[1] // width_kv
    scaling = 1.0 / math.sqrt(width_qk)
    highest_p = lax.Precision.HIGHEST
    me_ctx = lax.axis_index("ctx")
    me_head = lax.axis_index("head")

    blocks, sources = gather_ctx(latents, ctx_size)
    piece = blocks.reshape(ctx_size * rows_here, latents.shape[1])
    token_rows = (sources[:, None] * rows_here + jnp.arange(rows_here, dtype=jnp.int32)[None, :]).reshape(-1)

    queries3 = queries.reshape(rows_here, heads_here, width_qk)
    query_nope = queries3[:, :, :HEAD_DIM].astype(jnp.float32)
    query_rope = queries3[:, :, HEAD_DIM:]
    query_rows = me_ctx * rows_here + jnp.arange(rows_here, dtype=jnp.int32)
    query_pos = positions_of(block_order, query_rows, half_rows)

    row_count = piece.shape[0]
    packed = jnp.dot(piece[:, :LATENT], w_kv_up, preferred_element_type=jnp.float32)
    packed = packed.reshape(row_count, heads_here, width_kv)
    scores = jnp.einsum("qhd,khd->qhk", query_nope, packed[:, :, :HEAD_DIM], precision=highest_p)
    scores = scores + jnp.einsum(
        "qhd,kd->qhk", query_rope, piece[:, LATENT:], preferred_element_type=jnp.float32
    )
    scores = scores * scaling
    visible = (positions_of(block_order, token_rows, half_rows)[None, :] <= query_pos[:, None])[:, None, :]
    scores = jnp.where(visible, scores, NEGATIVE)
    highest = jnp.max(scores, axis=2, keepdims=True)
    weights = jnp.where(visible, jnp.exp(scores - highest), 0.0)
    totals = jnp.sum(weights, axis=2, keepdims=True)
    widened = lax.optimization_barrier(weights.astype(jnp.bfloat16)).astype(jnp.float32)
    mixed = jnp.einsum("qhk,khd->qhd", widened, packed[:, :, HEAD_DIM:], precision=highest_p)
    outputs = (mixed / totals).astype(jnp.bfloat16).reshape(rows_here, heads_here * V_DIM)

    out_blocks, out_sources = gather_ctx(outputs, ctx_size)
    per_target = ctx_size // head_size
    if ctx_size > DIRECT_LIMIT:
        slot_of_block = jnp.arange(ctx_size, dtype=jnp.int32)
    else:
        slot_of_block = jnp.stack([partner_of(me_ctx, block, ctx_size) for block in range(ctx_size)]).astype(jnp.int32)
    relative_targets = jnp.arange(head_size, dtype=jnp.int32) ^ me_head
    wanted_blocks = (relative_targets[:, None] * per_target + jnp.arange(per_target, dtype=jnp.int32)[None, :]).reshape(-1)
    ordered = jnp.take(out_blocks, slot_of_block[wanted_blocks], axis=0)
    ordered = ordered.reshape(head_size, per_target * rows_here, heads_here * V_DIM)
    partials = jnp.einsum("trf,fc->trc", ordered, w_out, preferred_element_type=jnp.float32)
    total = reduce_scatter_head(partials, head_size)
    return total.astype(jnp.bfloat16)


def solution(mesh):
    placed = (
        P(("grp", "ctx"), "head"),
        P(("grp", "ctx"), None),
        P(None, "head"),
        P("head", "ctx"),
        P("grp"),
    )
    body = lambda *args: on_device(*args, ctx_size=mesh.shape["ctx"], head_size=mesh.shape["head"])
    return jax.shard_map(
        body, mesh=mesh, in_specs=placed, out_specs=P(("grp", "head"), "ctx"), check_vma=False
    )
```

```python
import math

import jax
import jax.numpy as jnp
from jax import lax
from jax.sharding import PartitionSpec as P

LATENT = 256
ROPE = 64
HEAD_DIM = 64
V_DIM = 64

NEGATIVE = -1e30
DIRECT_LIMIT = 8


def positions_of(block_order, global_rows, half_rows):
    block_index = global_rows // half_rows
    matches = block_index[:, None] == jnp.arange(block_order.shape[0], dtype=jnp.int32)[None, :]
    picked = jnp.sum(jnp.where(matches, block_order[None, :], 0), axis=1)
    return picked * half_rows + global_rows % half_rows


def gather_ctx(x, ctx_size, relay=False):
    me = lax.axis_index("ctx")
    if ctx_size > DIRECT_LIMIT:
        whole = lax.all_gather(x, "ctx", axis=0, tiled=False)
        return whole, jnp.arange(ctx_size, dtype=jnp.int32)
    if relay and ctx_size == 4:
        near = lax.ppermute(x, "ctx", [(i ^ 1, i) for i in range(4)])
        far = lax.ppermute(x, "ctx", [(i ^ 2, i) for i in range(4)])
        relayed = lax.ppermute(far, "ctx", [(i ^ 1, i) for i in range(4)])
        sources = me ^ jnp.arange(4, dtype=jnp.int32)
        return jnp.stack([x, near, far, relayed]), sources
    pieces = [x]
    for step in range(1, ctx_size):
        pairs = [(partner_of(i, step, ctx_size), i) for i in range(ctx_size)]
        pieces.append(lax.ppermute(x, "ctx", pairs))
    sources = jnp.stack([partner_of(me, step, ctx_size) for step in range(ctx_size)]).astype(jnp.int32)
    return jnp.stack(pieces), sources


def partner_of(i, step, size):
    if size & (size - 1) == 0:
        return i ^ step
    return (i - step) % size


def reduce_scatter_head(relative, head_size):
    acc = relative
    bit = 1
    while bit < head_size:
        pairs = [(i, i ^ bit) for i in range(head_size)]
        grouped = acc.reshape((acc.shape[0] // 2, 2) + acc.shape[1:])
        kept = grouped[:, 0]
        sent = grouped[:, 1].astype(jnp.bfloat16)
        got = lax.ppermute(sent, "head", pairs)
        acc = kept + got.astype(jnp.float32)
        bit *= 2
    return acc[0]


def on_device(queries, latents, w_kv_up, w_out, block_order, *, ctx_size, head_size):
    rows_here = queries.shape[0]
    half_rows = rows_here // 2
    width_qk = HEAD_DIM + ROPE
    width_kv = HEAD_DIM + V_DIM
    heads_here = w_kv_up.shape[1] // width_kv
    scaling = 1.0 / math.sqrt(width_qk)
    highest_p = lax.Precision.HIGHEST
    me_ctx = lax.axis_index("ctx")
    me_head = lax.axis_index("head")

    blocks, sources = gather_ctx(latents, ctx_size)
    piece = blocks.reshape(ctx_size * rows_here, latents.shape[1])
    token_rows = (sources[:, None] * rows_here + jnp.arange(rows_here, dtype=jnp.int32)[None, :]).reshape(-1)

    queries3 = queries.reshape(rows_here, heads_here, width_qk)
    query_nope = queries3[:, :, :HEAD_DIM].astype(jnp.float32)
    query_rope = queries3[:, :, HEAD_DIM:]
    query_rows = me_ctx * rows_here + jnp.arange(rows_here, dtype=jnp.int32)
    query_pos = positions_of(block_order, query_rows, half_rows)

    row_count = piece.shape[0]
    packed = jnp.dot(piece[:, :LATENT], w_kv_up, preferred_element_type=jnp.float32)
    packed = packed.reshape(row_count, heads_here, width_kv)
    scores = jnp.einsum("qhd,khd->qhk", query_nope, packed[:, :, :HEAD_DIM], precision=highest_p)
    scores = scores + jnp.einsum(
        "qhd,kd->qhk", query_rope, piece[:, LATENT:], preferred_element_type=jnp.float32
    )
    scores = scores * scaling
    visible = (positions_of(block_order, token_rows, half_rows)[None, :] <= query_pos[:, None])[:, None, :]
    scores = jnp.where(visible, scores, NEGATIVE)
    highest = jnp.max(scores, axis=2, keepdims=True)
    weights = jnp.where(visible, jnp.exp(scores - highest), 0.0)
    totals = jnp.sum(weights, axis=2, keepdims=True)
    widened = lax.optimization_barrier(weights.astype(jnp.bfloat16)).astype(jnp.float32)
    mixed = jnp.einsum("qhk,khd->qhd", widened, packed[:, :, HEAD_DIM:], precision=highest_p)
    outputs = (mixed / totals).astype(jnp.bfloat16).reshape(rows_here, heads_here * V_DIM)

    out_blocks, out_sources = gather_ctx(outputs, ctx_size, relay=True)
    per_target = ctx_size // head_size
    if ctx_size > DIRECT_LIMIT:
        slot_of_block = jnp.arange(ctx_size, dtype=jnp.int32)
    else:
        slot_of_block = jnp.stack([partner_of(me_ctx, block, ctx_size) for block in range(ctx_size)]).astype(jnp.int32)
    relative_targets = jnp.arange(head_size, dtype=jnp.int32) ^ me_head
    wanted_blocks = (relative_targets[:, None] * per_target + jnp.arange(per_target, dtype=jnp.int32)[None, :]).reshape(-1)
    ordered = jnp.take(out_blocks, slot_of_block[wanted_blocks], axis=0)
    ordered = ordered.reshape(head_size, per_target * rows_here, heads_here * V_DIM)
    partials = jnp.einsum("trf,fc->trc", ordered, w_out, preferred_element_type=jnp.float32)
    total = reduce_scatter_head(partials, head_size)
    return total.astype(jnp.bfloat16)


def solution(mesh):
    placed = (
        P(("grp", "ctx"), "head"),
        P(("grp", "ctx"), None),
        P(None, "head"),
        P("head", "ctx"),
        P("grp"),
    )
    body = lambda *args: on_device(*args, ctx_size=mesh.shape["ctx"], head_size=mesh.shape["head"])
    return jax.shard_map(
        body, mesh=mesh, in_specs=placed, out_specs=P(("grp", "head"), "ctx"), check_vma=False
    )
```

```python
import math

import jax
import jax.numpy as jnp
from jax import lax
from jax.sharding import PartitionSpec as P

LATENT = 256
ROPE = 64
HEAD_DIM = 64
V_DIM = 64

NEGATIVE = -1e30
DIRECT_LIMIT = 8


def positions_of(block_order, global_rows, half_rows):
    block_index = global_rows // half_rows
    matches = block_index[:, None] == jnp.arange(block_order.shape[0], dtype=jnp.int32)[None, :]
    picked = jnp.sum(jnp.where(matches, block_order[None, :], 0), axis=1)
    return picked * half_rows + global_rows % half_rows


def gather_ctx(x, ctx_size, relay=False):
    me = lax.axis_index("ctx")
    if ctx_size > DIRECT_LIMIT:
        whole = lax.all_gather(x, "ctx", axis=0, tiled=False)
        return whole, jnp.arange(ctx_size, dtype=jnp.int32)
    if relay and ctx_size == 4:
        near = lax.ppermute(x, "ctx", [(i ^ 1, i) for i in range(4)])
        far = lax.ppermute(x, "ctx", [(i ^ 2, i) for i in range(4)])
        relayed = lax.ppermute(far, "ctx", [(i ^ 1, i) for i in range(4)])
        sources = me ^ jnp.arange(4, dtype=jnp.int32)
        return jnp.stack([x, near, far, relayed]), sources
    pieces = [x]
    for step in range(1, ctx_size):
        pairs = [(partner_of(i, step, ctx_size), i) for i in range(ctx_size)]
        pieces.append(lax.ppermute(x, "ctx", pairs))
    sources = jnp.stack([partner_of(me, step, ctx_size) for step in range(ctx_size)]).astype(jnp.int32)
    return jnp.stack(pieces), sources


def split_bf16(x):
    high = lax.reduce_precision(x, exponent_bits=8, mantissa_bits=7)
    rest = x - high
    middle = lax.reduce_precision(rest, exponent_bits=8, mantissa_bits=7)
    low = rest - middle
    return [part.astype(jnp.bfloat16) for part in (high, middle, low)]


def partner_of(i, step, size):
    if size & (size - 1) == 0:
        return i ^ step
    return (i - step) % size


def reduce_scatter_head(relative, head_size):
    acc = relative
    bit = 1
    while bit < head_size:
        pairs = [(i, i ^ bit) for i in range(head_size)]
        grouped = acc.reshape((acc.shape[0] // 2, 2) + acc.shape[1:])
        kept = grouped[:, 0]
        sent = grouped[:, 1].astype(jnp.bfloat16)
        got = lax.ppermute(sent, "head", pairs)
        acc = kept + got.astype(jnp.float32)
        bit *= 2
    return acc[0]


def on_device(queries, latents, w_kv_up, w_out, block_order, *, ctx_size, head_size):
    rows_here = queries.shape[0]
    half_rows = rows_here // 2
    width_qk = HEAD_DIM + ROPE
    width_kv = HEAD_DIM + V_DIM
    heads_here = w_kv_up.shape[1] // width_kv
    scaling = 1.0 / math.sqrt(width_qk)
    highest_p = lax.Precision.HIGHEST
    me_ctx = lax.axis_index("ctx")
    me_head = lax.axis_index("head")

    blocks, sources = gather_ctx(latents, ctx_size)
    piece = blocks.reshape(ctx_size * rows_here, latents.shape[1])
    token_rows = (sources[:, None] * rows_here + jnp.arange(rows_here, dtype=jnp.int32)[None, :]).reshape(-1)

    queries3 = queries.reshape(rows_here, heads_here, width_qk)
    query_nope_bf16 = queries3[:, :, :HEAD_DIM]
    query_rope = queries3[:, :, HEAD_DIM:]
    query_rows = me_ctx * rows_here + jnp.arange(rows_here, dtype=jnp.int32)
    query_pos = positions_of(block_order, query_rows, half_rows)

    row_count = piece.shape[0]
    packed = jnp.dot(piece[:, :LATENT], w_kv_up, preferred_element_type=jnp.float32)
    packed = packed.reshape(row_count, heads_here, width_kv)
    key_parts = split_bf16(packed[:, :, :HEAD_DIM])
    value_parts = split_bf16(packed[:, :, HEAD_DIM:])
    rotary = jnp.broadcast_to(piece[:, None, LATENT:], (row_count, heads_here, ROPE))
    keys_wide = jnp.concatenate(key_parts + [rotary], axis=2)
    queries_wide = jnp.concatenate([query_nope_bf16] * 3 + [query_rope], axis=2)
    scores = jnp.einsum("qhd,khd->qhk", queries_wide, keys_wide, preferred_element_type=jnp.float32)
    scores = scores * scaling
    visible = (positions_of(block_order, token_rows, half_rows)[None, :] <= query_pos[:, None])[:, None, :]
    scores = jnp.where(visible, scores, NEGATIVE)
    highest = jnp.max(scores, axis=2, keepdims=True)
    weights = jnp.where(visible, jnp.exp(scores - highest), 0.0)
    totals = jnp.sum(weights, axis=2, keepdims=True)
    rounded = lax.optimization_barrier(weights.astype(jnp.bfloat16))
    values_wide = jnp.concatenate(value_parts, axis=2)
    mixed_parts = jnp.einsum("qhk,khd->qhd", rounded, values_wide, preferred_element_type=jnp.float32)
    mixed = (mixed_parts[:, :, :V_DIM] + mixed_parts[:, :, V_DIM:2 * V_DIM]) + mixed_parts[:, :, 2 * V_DIM:]
    outputs = (mixed / totals).astype(jnp.bfloat16).reshape(rows_here, heads_here * V_DIM)

    out_blocks, out_sources = gather_ctx(outputs, ctx_size, relay=True)
    per_target = ctx_size // head_size
    if ctx_size > DIRECT_LIMIT:
        slot_of_block = jnp.arange(ctx_size, dtype=jnp.int32)
    else:
        slot_of_block = jnp.stack([partner_of(me_ctx, block, ctx_size) for block in range(ctx_size)]).astype(jnp.int32)
    relative_targets = jnp.arange(head_size, dtype=jnp.int32) ^ me_head
    wanted_blocks = (relative_targets[:, None] * per_target + jnp.arange(per_target, dtype=jnp.int32)[None, :]).reshape(-1)
    ordered = jnp.take(out_blocks, slot_of_block[wanted_blocks], axis=0)
    ordered = ordered.reshape(head_size, per_target * rows_here, heads_here * V_DIM)
    partials = jnp.einsum("trf,fc->trc", ordered, w_out, preferred_element_type=jnp.float32)
    total = reduce_scatter_head(partials, head_size)
    return total.astype(jnp.bfloat16)


def solution(mesh):
    placed = (
        P(("grp", "ctx"), "head"),
        P(("grp", "ctx"), None),
        P(None, "head"),
        P("head", "ctx"),
        P("grp"),
    )
    body = lambda *args: on_device(*args, ctx_size=mesh.shape["ctx"], head_size=mesh.shape["head"])
    return jax.shard_map(
        body, mesh=mesh, in_specs=placed, out_specs=P(("grp", "head"), "ctx"), check_vma=False
    )
```

```python
import math

import jax
import jax.numpy as jnp
from jax import lax
from jax.sharding import PartitionSpec as P

LATENT = 256
ROPE = 64
HEAD_DIM = 64
V_DIM = 64

NEGATIVE = -1e30
DIRECT_LIMIT = 8


def gather_ctx(x, ctx_size, relay=False):
    me = lax.axis_index("ctx")
    if ctx_size > DIRECT_LIMIT:
        whole = lax.all_gather(x, "ctx", axis=0, tiled=False)
        return whole, jnp.arange(ctx_size, dtype=jnp.int32)
    if relay and ctx_size == 4:
        near = lax.ppermute(x, "ctx", [(i ^ 1, i) for i in range(4)])
        far = lax.ppermute(x, "ctx", [(i ^ 2, i) for i in range(4)])
        relayed = lax.ppermute(far, "ctx", [(i ^ 1, i) for i in range(4)])
        sources = me ^ jnp.arange(4, dtype=jnp.int32)
        return jnp.stack([x, near, far, relayed]), sources
    pieces = [x]
    for step in range(1, ctx_size):
        pairs = [(partner_of(i, step, ctx_size), i) for i in range(ctx_size)]
        pieces.append(lax.ppermute(x, "ctx", pairs))
    sources = jnp.stack([partner_of(me, step, ctx_size) for step in range(ctx_size)]).astype(jnp.int32)
    return jnp.stack(pieces), sources


def partner_of(i, step, size):
    if size & (size - 1) == 0:
        return i ^ step
    return (i - step) % size


def reduce_scatter_head(relative, head_size):
    acc = relative
    bit = 1
    while bit < head_size:
        pairs = [(i, i ^ bit) for i in range(head_size)]
        grouped = acc.reshape((acc.shape[0] // 2, 2) + acc.shape[1:])
        kept = grouped[:, 0]
        sent = grouped[:, 1].astype(jnp.bfloat16)
        got = lax.ppermute(sent, "head", pairs)
        acc = kept + got.astype(jnp.float32)
        bit *= 2
    return acc[0]


def on_device(queries, latents, w_kv_up, w_out, block_order, *, ctx_size, head_size):
    rows_here = queries.shape[0]
    half_rows = rows_here // 2
    width_qk = HEAD_DIM + ROPE
    width_kv = HEAD_DIM + V_DIM
    heads_here = w_kv_up.shape[1] // width_kv
    scaling = 1.0 / math.sqrt(width_qk)
    highest_p = lax.Precision.HIGHEST
    me_ctx = lax.axis_index("ctx")
    me_head = lax.axis_index("head")

    blocks, sources = gather_ctx(latents, ctx_size)
    piece = blocks.reshape(ctx_size * rows_here, latents.shape[1])
    per_piece = rows_here // half_rows
    order_blocks = block_order.reshape(ctx_size, per_piece)
    source_match = sources[:, None, None] == jnp.arange(ctx_size, dtype=jnp.int32)[None, :, None]
    piece_order = jnp.sum(jnp.where(source_match, order_blocks[None, :, :], 0), axis=1)
    in_block = jnp.arange(half_rows, dtype=jnp.int32)
    key_pos = (piece_order[:, :, None] * half_rows + in_block[None, None, :]).reshape(-1)
    own_order = lax.dynamic_index_in_dim(order_blocks, me_ctx, 0, keepdims=False)
    query_pos = (own_order[:, None] * half_rows + in_block[None, :]).reshape(-1)

    queries3 = queries.reshape(rows_here, heads_here, width_qk)
    query_nope = queries3[:, :, :HEAD_DIM].astype(jnp.float32)
    query_rope = queries3[:, :, HEAD_DIM:]

    row_count = piece.shape[0]
    packed = jnp.dot(piece[:, :LATENT], w_kv_up, preferred_element_type=jnp.float32)
    packed = packed.reshape(row_count, heads_here, width_kv)
    scores = jnp.einsum("qhd,khd->qhk", query_nope, packed[:, :, :HEAD_DIM], precision=highest_p)
    scores = scores + jnp.einsum(
        "qhd,kd->qhk", query_rope, piece[:, LATENT:], preferred_element_type=jnp.float32
    )
    scores = scores * scaling
    visible = (key_pos[None, :] <= query_pos[:, None])[:, None, :]
    scores = jnp.where(visible, scores, NEGATIVE)
    highest = jnp.max(scores, axis=2, keepdims=True)
    weights = jnp.where(visible, jnp.exp(scores - highest), 0.0)
    totals = jnp.sum(weights, axis=2, keepdims=True)
    widened = lax.optimization_barrier(weights.astype(jnp.bfloat16)).astype(jnp.float32)
    mixed = jnp.einsum("qhk,khd->qhd", widened, packed[:, :, HEAD_DIM:], precision=highest_p)
    outputs = (mixed / totals).astype(jnp.bfloat16).reshape(rows_here, heads_here * V_DIM)

    out_blocks, out_sources = gather_ctx(outputs, ctx_size, relay=True)
    per_target = ctx_size // head_size
    if ctx_size > DIRECT_LIMIT:
        slot_of_block = jnp.arange(ctx_size, dtype=jnp.int32)
    else:
        slot_of_block = jnp.stack([partner_of(me_ctx, block, ctx_size) for block in range(ctx_size)]).astype(jnp.int32)
    relative_targets = jnp.arange(head_size, dtype=jnp.int32) ^ me_head
    wanted_blocks = (relative_targets[:, None] * per_target + jnp.arange(per_target, dtype=jnp.int32)[None, :]).reshape(-1)
    if ctx_size == head_size and ctx_size <= DIRECT_LIMIT and ctx_size & (ctx_size - 1) == 0:
        wanted_slots = jnp.arange(head_size, dtype=jnp.int32) ^ (me_ctx ^ me_head)
    else:
        wanted_slots = slot_of_block[wanted_blocks]
    ordered = jnp.take(out_blocks, wanted_slots, axis=0)
    ordered = ordered.reshape(head_size, per_target * rows_here, heads_here * V_DIM)
    partials = jnp.einsum("trf,fc->trc", ordered, w_out, preferred_element_type=jnp.float32)
    total = reduce_scatter_head(partials, head_size)
    return total.astype(jnp.bfloat16)


def solution(mesh):
    placed = (
        P(("grp", "ctx"), "head"),
        P(("grp", "ctx"), None),
        P(None, "head"),
        P("head", "ctx"),
        P("grp"),
    )
    body = lambda *args: on_device(*args, ctx_size=mesh.shape["ctx"], head_size=mesh.shape["head"])
    return jax.shard_map(
        body, mesh=mesh, in_specs=placed, out_specs=P(("grp", "head"), "ctx"), check_vma=False
    )
```

```python
import math

import jax
import jax.numpy as jnp
from jax import lax
from jax.sharding import PartitionSpec as P

LATENT = 256
ROPE = 64
HEAD_DIM = 64
V_DIM = 64

NEGATIVE = -1e30
DIRECT_LIMIT = 8


def gather_ctx(x, ctx_size, relay=False):
    me = lax.axis_index("ctx")
    if ctx_size > DIRECT_LIMIT:
        whole = lax.all_gather(x, "ctx", axis=0, tiled=False)
        return whole, jnp.arange(ctx_size, dtype=jnp.int32)
    if relay and ctx_size == 4:
        near = lax.ppermute(x, "ctx", [(i ^ 1, i) for i in range(4)])
        far = lax.ppermute(x, "ctx", [(i ^ 2, i) for i in range(4)])
        relayed = lax.ppermute(far, "ctx", [(i ^ 1, i) for i in range(4)])
        sources = me ^ jnp.arange(4, dtype=jnp.int32)
        return jnp.stack([x, near, far, relayed]), sources
    pieces = [x]
    for step in range(1, ctx_size):
        pairs = [(partner_of(i, step, ctx_size), i) for i in range(ctx_size)]
        pieces.append(lax.ppermute(x, "ctx", pairs))
    sources = jnp.stack([partner_of(me, step, ctx_size) for step in range(ctx_size)]).astype(jnp.int32)
    return jnp.stack(pieces), sources


def partner_of(i, step, size):
    if size & (size - 1) == 0:
        return i ^ step
    return (i - step) % size


def reduce_scatter_head(relative, head_size):
    acc = relative
    bit = 1
    while bit < head_size:
        pairs = [(i, i ^ bit) for i in range(head_size)]
        grouped = acc.reshape((acc.shape[0] // 2, 2) + acc.shape[1:])
        kept = grouped[:, 0]
        sent = grouped[:, 1].astype(jnp.bfloat16)
        got = lax.ppermute(sent, "head", pairs)
        acc = kept + got.astype(jnp.float32)
        bit *= 2
    return acc[0]


def on_device(queries, latents, w_kv_up, w_out, block_order, *, ctx_size, head_size):
    rows_here = queries.shape[0]
    half_rows = rows_here // 2
    width_qk = HEAD_DIM + ROPE
    width_kv = HEAD_DIM + V_DIM
    heads_here = w_kv_up.shape[1] // width_kv
    scaling = 1.0 / math.sqrt(width_qk)
    highest_p = lax.Precision.HIGHEST
    me_ctx = lax.axis_index("ctx")
    me_head = lax.axis_index("head")

    blocks, sources = gather_ctx(latents, ctx_size)
    piece = blocks.reshape(ctx_size * rows_here, latents.shape[1])
    per_piece = rows_here // half_rows
    in_piece = jnp.arange(per_piece, dtype=jnp.int32)
    all_blocks = jnp.arange(block_order.shape[0], dtype=jnp.int32)

    def order_of(block_index):
        matches = block_index[..., None] == all_blocks
        return jnp.sum(jnp.where(matches, block_order, 0), axis=-1)

    piece_order = order_of(sources[:, None] * per_piece + in_piece[None, :])
    in_block = jnp.arange(half_rows, dtype=jnp.int32)
    key_pos = (piece_order[:, :, None] * half_rows + in_block[None, None, :]).reshape(-1)
    own_order = order_of(me_ctx * per_piece + in_piece)
    query_pos = (own_order[:, None] * half_rows + in_block[None, :]).reshape(-1)

    queries3 = queries.reshape(rows_here, heads_here, width_qk)
    query_nope = queries3[:, :, :HEAD_DIM].astype(jnp.float32)
    query_rope = queries3[:, :, HEAD_DIM:]

    row_count = piece.shape[0]
    packed = jnp.dot(piece[:, :LATENT], w_kv_up, preferred_element_type=jnp.float32)
    packed = packed.reshape(row_count, heads_here, width_kv)
    scores = jnp.einsum("qhd,khd->qhk", query_nope, packed[:, :, :HEAD_DIM], precision=highest_p)
    scores = scores + jnp.einsum(
        "qhd,kd->qhk", query_rope, piece[:, LATENT:], preferred_element_type=jnp.float32
    )
    scores = scores * scaling
    visible = (key_pos[None, :] <= query_pos[:, None])[:, None, :]
    scores = jnp.where(visible, scores, NEGATIVE)
    highest = jnp.max(scores, axis=2, keepdims=True)
    weights = jnp.where(visible, jnp.exp(scores - highest), 0.0)
    totals = jnp.sum(weights, axis=2, keepdims=True)
    widened = lax.optimization_barrier(weights.astype(jnp.bfloat16)).astype(jnp.float32)
    mixed = jnp.einsum("qhk,khd->qhd", widened, packed[:, :, HEAD_DIM:], precision=highest_p)
    outputs = (mixed / totals).astype(jnp.bfloat16).reshape(rows_here, heads_here * V_DIM)

    out_blocks, out_sources = gather_ctx(outputs, ctx_size, relay=True)
    per_target = ctx_size // head_size
    if ctx_size > DIRECT_LIMIT:
        slot_of_block = jnp.arange(ctx_size, dtype=jnp.int32)
    else:
        slot_of_block = jnp.stack([partner_of(me_ctx, block, ctx_size) for block in range(ctx_size)]).astype(jnp.int32)
    relative_targets = jnp.arange(head_size, dtype=jnp.int32) ^ me_head
    wanted_blocks = (relative_targets[:, None] * per_target + jnp.arange(per_target, dtype=jnp.int32)[None, :]).reshape(-1)
    if ctx_size == head_size and ctx_size <= DIRECT_LIMIT and ctx_size & (ctx_size - 1) == 0:
        wanted_slots = jnp.arange(head_size, dtype=jnp.int32) ^ (me_ctx ^ me_head)
    else:
        wanted_slots = slot_of_block[wanted_blocks]
    ordered = jnp.take(out_blocks, wanted_slots, axis=0)
    ordered = ordered.reshape(head_size, per_target * rows_here, heads_here * V_DIM)
    partials = jnp.einsum("trf,fc->trc", ordered, w_out, preferred_element_type=jnp.float32)
    total = reduce_scatter_head(partials, head_size)
    return total.astype(jnp.bfloat16)


def solution(mesh):
    placed = (
        P(("grp", "ctx"), "head"),
        P(("grp", "ctx"), None),
        P(None, "head"),
        P("head", "ctx"),
        P("grp"),
    )
    body = lambda *args: on_device(*args, ctx_size=mesh.shape["ctx"], head_size=mesh.shape["head"])
    return jax.shard_map(
        body, mesh=mesh, in_specs=placed, out_specs=P(("grp", "head"), "ctx"), check_vma=False
    )
```

```python
import math

import jax
import jax.numpy as jnp
from jax import lax
from jax.sharding import PartitionSpec as P

LATENT = 256
ROPE = 64
HEAD_DIM = 64
V_DIM = 64

NEGATIVE = -1e30
DIRECT_LIMIT = 8


def positions_of(block_order, global_rows, half_rows):
    block_index = global_rows // half_rows
    matches = block_index[:, None] == jnp.arange(block_order.shape[0], dtype=jnp.int32)[None, :]
    picked = jnp.sum(jnp.where(matches, block_order[None, :], 0), axis=1)
    return picked * half_rows + global_rows % half_rows


def gather_ctx(x, ctx_size, relay=False, doubling=False):
    me = lax.axis_index("ctx")
    if ctx_size > DIRECT_LIMIT:
        whole = lax.all_gather(x, "ctx", axis=0, tiled=False)
        return whole, jnp.arange(ctx_size, dtype=jnp.int32)
    if doubling and ctx_size & (ctx_size - 1) == 0:
        held = x[None]
        bit = 1
        while bit < ctx_size:
            got = lax.ppermute(held, "ctx", [(i ^ bit, i) for i in range(ctx_size)])
            held = jnp.concatenate([held, got], axis=0)
            bit *= 2
        return held, me ^ jnp.arange(ctx_size, dtype=jnp.int32)
    if relay and ctx_size == 4:
        near = lax.ppermute(x, "ctx", [(i ^ 1, i) for i in range(4)])
        far = lax.ppermute(x, "ctx", [(i ^ 2, i) for i in range(4)])
        relayed = lax.ppermute(far, "ctx", [(i ^ 1, i) for i in range(4)])
        sources = me ^ jnp.arange(4, dtype=jnp.int32)
        return jnp.stack([x, near, far, relayed]), sources
    pieces = [x]
    for step in range(1, ctx_size):
        pairs = [(partner_of(i, step, ctx_size), i) for i in range(ctx_size)]
        pieces.append(lax.ppermute(x, "ctx", pairs))
    sources = jnp.stack([partner_of(me, step, ctx_size) for step in range(ctx_size)]).astype(jnp.int32)
    return jnp.stack(pieces), sources


def partner_of(i, step, size):
    if size & (size - 1) == 0:
        return i ^ step
    return (i - step) % size


def reduce_scatter_head(relative, head_size):
    acc = relative
    bit = 1
    while bit < head_size:
        pairs = [(i, i ^ bit) for i in range(head_size)]
        grouped = acc.reshape((acc.shape[0] // 2, 2) + acc.shape[1:])
        kept = grouped[:, 0]
        sent = grouped[:, 1].astype(jnp.bfloat16)
        got = lax.ppermute(sent, "head", pairs)
        acc = kept + got.astype(jnp.float32)
        bit *= 2
    return acc[0]


def on_device(queries, latents, w_kv_up, w_out, block_order, *, ctx_size, head_size):
    rows_here = queries.shape[0]
    half_rows = rows_here // 2
    width_qk = HEAD_DIM + ROPE
    width_kv = HEAD_DIM + V_DIM
    heads_here = w_kv_up.shape[1] // width_kv
    scaling = 1.0 / math.sqrt(width_qk)
    highest_p = lax.Precision.HIGHEST
    me_ctx = lax.axis_index("ctx")
    me_head = lax.axis_index("head")

    blocks, sources = gather_ctx(latents, ctx_size, doubling=True)
    piece = blocks.reshape(ctx_size * rows_here, latents.shape[1])
    token_rows = (sources[:, None] * rows_here + jnp.arange(rows_here, dtype=jnp.int32)[None, :]).reshape(-1)

    queries3 = queries.reshape(rows_here, heads_here, width_qk)
    query_nope = queries3[:, :, :HEAD_DIM].astype(jnp.float32)
    query_rope = queries3[:, :, HEAD_DIM:]
    query_rows = me_ctx * rows_here + jnp.arange(rows_here, dtype=jnp.int32)
    query_pos = positions_of(block_order, query_rows, half_rows)

    row_count = piece.shape[0]
    packed = jnp.dot(piece[:, :LATENT], w_kv_up, preferred_element_type=jnp.float32)
    packed = packed.reshape(row_count, heads_here, width_kv)
    scores = jnp.einsum("qhd,khd->qhk", query_nope, packed[:, :, :HEAD_DIM], precision=highest_p)
    scores = scores + jnp.einsum(
        "qhd,kd->qhk", query_rope, piece[:, LATENT:], preferred_element_type=jnp.float32
    )
    scores = scores * scaling
    visible = (positions_of(block_order, token_rows, half_rows)[None, :] <= query_pos[:, None])[:, None, :]
    scores = jnp.where(visible, scores, NEGATIVE)
    highest = jnp.max(scores, axis=2, keepdims=True)
    weights = jnp.where(visible, jnp.exp(scores - highest), 0.0)
    totals = jnp.sum(weights, axis=2, keepdims=True)
    widened = lax.optimization_barrier(weights.astype(jnp.bfloat16)).astype(jnp.float32)
    mixed = jnp.einsum("qhk,khd->qhd", widened, packed[:, :, HEAD_DIM:], precision=highest_p)
    outputs = (mixed / totals).astype(jnp.bfloat16).reshape(rows_here, heads_here * V_DIM)

    out_blocks, out_sources = gather_ctx(outputs, ctx_size, relay=True)
    per_target = ctx_size // head_size
    if ctx_size > DIRECT_LIMIT:
        slot_of_block = jnp.arange(ctx_size, dtype=jnp.int32)
    else:
        slot_of_block = jnp.stack([partner_of(me_ctx, block, ctx_size) for block in range(ctx_size)]).astype(jnp.int32)
    relative_targets = jnp.arange(head_size, dtype=jnp.int32) ^ me_head
    wanted_blocks = (relative_targets[:, None] * per_target + jnp.arange(per_target, dtype=jnp.int32)[None, :]).reshape(-1)
    ordered = jnp.take(out_blocks, slot_of_block[wanted_blocks], axis=0)
    ordered = ordered.reshape(head_size, per_target * rows_here, heads_here * V_DIM)
    partials = jnp.einsum("trf,fc->trc", ordered, w_out, preferred_element_type=jnp.float32)
    total = reduce_scatter_head(partials, head_size)
    return total.astype(jnp.bfloat16)


def solution(mesh):
    placed = (
        P(("grp", "ctx"), "head"),
        P(("grp", "ctx"), None),
        P(None, "head"),
        P("head", "ctx"),
        P("grp"),
    )
    body = lambda *args: on_device(*args, ctx_size=mesh.shape["ctx"], head_size=mesh.shape["head"])
    return jax.shard_map(
        body, mesh=mesh, in_specs=placed, out_specs=P(("grp", "head"), "ctx"), check_vma=False
    )
```

```python
import math

import jax
import jax.numpy as jnp
from jax import lax
from jax.sharding import PartitionSpec as P

LATENT = 256
ROPE = 64
HEAD_DIM = 64
V_DIM = 64

NEGATIVE = -1e30
DIRECT_LIMIT = 8


def positions_of(block_order, global_rows, half_rows):
    block_index = global_rows // half_rows
    matches = block_index[:, None] == jnp.arange(block_order.shape[0], dtype=jnp.int32)[None, :]
    picked = jnp.sum(jnp.where(matches, block_order[None, :], 0), axis=1)
    return picked * half_rows + global_rows % half_rows


def gather_ctx(x, ctx_size, relay=False):
    me = lax.axis_index("ctx")
    if ctx_size > DIRECT_LIMIT:
        whole = lax.all_gather(x, "ctx", axis=0, tiled=False)
        return whole, jnp.arange(ctx_size, dtype=jnp.int32)
    if relay and ctx_size == 4:
        near = lax.ppermute(x, "ctx", [(i ^ 1, i) for i in range(4)])
        far = lax.ppermute(x, "ctx", [(i ^ 2, i) for i in range(4)])
        relayed = lax.ppermute(far, "ctx", [(i ^ 1, i) for i in range(4)])
        sources = me ^ jnp.arange(4, dtype=jnp.int32)
        return jnp.stack([x, near, far, relayed]), sources
    pieces = [x]
    for step in range(1, ctx_size):
        pairs = [(partner_of(i, step, ctx_size), i) for i in range(ctx_size)]
        pieces.append(lax.ppermute(x, "ctx", pairs))
    sources = jnp.stack([partner_of(me, step, ctx_size) for step in range(ctx_size)]).astype(jnp.int32)
    return jnp.stack(pieces), sources


def partner_of(i, step, size):
    if size & (size - 1) == 0:
        return i ^ step
    return (i - step) % size


def reduce_scatter_head(relative, head_size):
    acc = relative
    bit = 1
    while bit < head_size:
        pairs = [(i, i ^ bit) for i in range(head_size)]
        grouped = acc.reshape((acc.shape[0] // 2, 2) + acc.shape[1:])
        kept = grouped[:, 0]
        sent = grouped[:, 1].astype(jnp.bfloat16)
        if bit > 1 and sent.shape[-1] % 256 == 0:
            half = sent.shape[-1] // 2
            got = jnp.concatenate(
                [lax.ppermute(sent[..., :half], "head", pairs), lax.ppermute(sent[..., half:], "head", pairs)],
                axis=-1,
            )
        else:
            got = lax.ppermute(sent, "head", pairs)
        acc = kept + got.astype(jnp.float32)
        bit *= 2
    return acc[0]


def on_device(queries, latents, w_kv_up, w_out, block_order, *, ctx_size, head_size):
    rows_here = queries.shape[0]
    half_rows = rows_here // 2
    width_qk = HEAD_DIM + ROPE
    width_kv = HEAD_DIM + V_DIM
    heads_here = w_kv_up.shape[1] // width_kv
    scaling = 1.0 / math.sqrt(width_qk)
    highest_p = lax.Precision.HIGHEST
    me_ctx = lax.axis_index("ctx")
    me_head = lax.axis_index("head")

    blocks, sources = gather_ctx(latents, ctx_size)
    piece = blocks.reshape(ctx_size * rows_here, latents.shape[1])
    token_rows = (sources[:, None] * rows_here + jnp.arange(rows_here, dtype=jnp.int32)[None, :]).reshape(-1)

    queries3 = queries.reshape(rows_here, heads_here, width_qk)
    query_nope = queries3[:, :, :HEAD_DIM].astype(jnp.float32)
    query_rope = queries3[:, :, HEAD_DIM:]
    query_rows = me_ctx * rows_here + jnp.arange(rows_here, dtype=jnp.int32)
    query_pos = positions_of(block_order, query_rows, half_rows)

    row_count = piece.shape[0]
    packed = jnp.dot(piece[:, :LATENT], w_kv_up, preferred_element_type=jnp.float32)
    packed = packed.reshape(row_count, heads_here, width_kv)
    scores = jnp.einsum("qhd,khd->qhk", query_nope, packed[:, :, :HEAD_DIM], precision=highest_p)
    scores = scores + jnp.einsum(
        "qhd,kd->qhk", query_rope, piece[:, LATENT:], preferred_element_type=jnp.float32
    )
    scores = scores * scaling
    visible = (positions_of(block_order, token_rows, half_rows)[None, :] <= query_pos[:, None])[:, None, :]
    scores = jnp.where(visible, scores, NEGATIVE)
    highest = jnp.max(scores, axis=2, keepdims=True)
    weights = jnp.where(visible, jnp.exp(scores - highest), 0.0)
    totals = jnp.sum(weights, axis=2, keepdims=True)
    widened = lax.optimization_barrier(weights.astype(jnp.bfloat16)).astype(jnp.float32)
    mixed = jnp.einsum("qhk,khd->qhd", widened, packed[:, :, HEAD_DIM:], precision=highest_p)
    outputs = (mixed / totals).astype(jnp.bfloat16).reshape(rows_here, heads_here * V_DIM)

    out_blocks, out_sources = gather_ctx(outputs, ctx_size, relay=True)
    per_target = ctx_size // head_size
    if ctx_size > DIRECT_LIMIT:
        slot_of_block = jnp.arange(ctx_size, dtype=jnp.int32)
    else:
        slot_of_block = jnp.stack([partner_of(me_ctx, block, ctx_size) for block in range(ctx_size)]).astype(jnp.int32)
    relative_targets = jnp.arange(head_size, dtype=jnp.int32) ^ me_head
    wanted_blocks = (relative_targets[:, None] * per_target + jnp.arange(per_target, dtype=jnp.int32)[None, :]).reshape(-1)
    ordered = jnp.take(out_blocks, slot_of_block[wanted_blocks], axis=0)
    ordered = ordered.reshape(head_size, per_target * rows_here, heads_here * V_DIM)
    partials = jnp.einsum("trf,fc->trc", ordered, w_out, preferred_element_type=jnp.float32)
    total = reduce_scatter_head(partials, head_size)
    return total.astype(jnp.bfloat16)


def solution(mesh):
    placed = (
        P(("grp", "ctx"), "head"),
        P(("grp", "ctx"), None),
        P(None, "head"),
        P("head", "ctx"),
        P("grp"),
    )
    body = lambda *args: on_device(*args, ctx_size=mesh.shape["ctx"], head_size=mesh.shape["head"])
    return jax.shard_map(
        body, mesh=mesh, in_specs=placed, out_specs=P(("grp", "head"), "ctx"), check_vma=False
    )
```

```python
import math

import jax
import jax.numpy as jnp
from jax import lax
from jax.sharding import PartitionSpec as P

LATENT = 256
ROPE = 64
HEAD_DIM = 64
V_DIM = 64

NEGATIVE = -1e30
DIRECT_LIMIT = 8


def positions_of(block_order, global_rows, half_rows):
    block_index = global_rows // half_rows
    matches = block_index[:, None] == jnp.arange(block_order.shape[0], dtype=jnp.int32)[None, :]
    picked = jnp.sum(jnp.where(matches, block_order[None, :], 0), axis=1)
    return picked * half_rows + global_rows % half_rows


def gather_ctx(x, ctx_size, relay=False):
    me = lax.axis_index("ctx")
    if ctx_size > DIRECT_LIMIT:
        whole = lax.all_gather(x, "ctx", axis=0, tiled=False)
        return whole, jnp.arange(ctx_size, dtype=jnp.int32)
    if relay and ctx_size == 4:
        near = lax.ppermute(x, "ctx", [(i ^ 1, i) for i in range(4)])
        far = lax.ppermute(x, "ctx", [(i ^ 2, i) for i in range(4)])
        relayed = lax.ppermute(far, "ctx", [(i ^ 1, i) for i in range(4)])
        sources = me ^ jnp.arange(4, dtype=jnp.int32)
        return jnp.stack([x, near, far, relayed]), sources
    pieces = [x]
    for step in range(1, ctx_size):
        pairs = [(partner_of(i, step, ctx_size), i) for i in range(ctx_size)]
        pieces.append(lax.ppermute(x, "ctx", pairs))
    sources = jnp.stack([partner_of(me, step, ctx_size) for step in range(ctx_size)]).astype(jnp.int32)
    return jnp.stack(pieces), sources


def partner_of(i, step, size):
    if size & (size - 1) == 0:
        return i ^ step
    return (i - step) % size


def reduce_scatter_head(relative, head_size):
    acc = relative
    bit = 1
    while bit < head_size:
        pairs = [(i, i ^ bit) for i in range(head_size)]
        grouped = acc.reshape((acc.shape[0] // 2, 2) + acc.shape[1:])
        kept = grouped[:, 0]
        sent = grouped[:, 1].astype(jnp.bfloat16)
        got = lax.ppermute(sent, "head", pairs)
        acc = kept + got.astype(jnp.float32)
        bit *= 2
    return acc[0]


def on_device(queries, latents, w_kv_up, w_out, block_order, *, ctx_size, head_size):
    rows_here = queries.shape[0]
    half_rows = rows_here // 2
    width_qk = HEAD_DIM + ROPE
    width_kv = HEAD_DIM + V_DIM
    heads_here = w_kv_up.shape[1] // width_kv
    scaling = 1.0 / math.sqrt(width_qk)
    highest_p = lax.Precision.HIGHEST
    me_ctx = lax.axis_index("ctx")
    me_head = lax.axis_index("head")

    blocks, sources = gather_ctx(latents, ctx_size)
    piece = blocks.reshape(ctx_size * rows_here, latents.shape[1])
    token_rows = (sources[:, None] * rows_here + jnp.arange(rows_here, dtype=jnp.int32)[None, :]).reshape(-1)

    queries3 = queries.reshape(rows_here, heads_here, width_qk)
    query_nope = queries3[:, :, :HEAD_DIM].astype(jnp.float32)
    query_rope = queries3[:, :, HEAD_DIM:]
    query_rows = me_ctx * rows_here + jnp.arange(rows_here, dtype=jnp.int32)
    query_pos = positions_of(block_order, query_rows, half_rows)

    row_count = piece.shape[0]
    packed = jnp.dot(piece[:, :LATENT], w_kv_up, preferred_element_type=jnp.float32)
    packed = packed.reshape(row_count, heads_here, width_kv)
    scores = jnp.einsum("qhd,khd->qhk", query_nope, packed[:, :, :HEAD_DIM], precision=highest_p)
    scores = scores + jnp.einsum(
        "qhd,kd->qhk", query_rope, piece[:, LATENT:], preferred_element_type=jnp.float32
    )
    scores = scores * scaling
    visible = (positions_of(block_order, token_rows, half_rows)[None, :] <= query_pos[:, None])[:, None, :]
    scores = jnp.where(visible, scores, NEGATIVE)
    highest = jnp.max(scores, axis=2, keepdims=True)
    weights = jnp.where(visible, jnp.exp(scores - highest), 0.0)
    totals = jnp.sum(weights, axis=2, keepdims=True)
    widened = lax.optimization_barrier(weights.astype(jnp.bfloat16)).astype(jnp.float32)
    mixed = jnp.einsum("qhk,khd->qhd", widened, packed[:, :, HEAD_DIM:], precision=highest_p)
    outputs = (mixed / totals).astype(jnp.bfloat16).reshape(rows_here, heads_here * V_DIM)

    out_blocks, out_sources = gather_ctx(outputs, ctx_size, relay=True)
    per_target = ctx_size // head_size
    if ctx_size > DIRECT_LIMIT:
        slot_of_block = jnp.arange(ctx_size, dtype=jnp.int32)
    else:
        slot_of_block = jnp.stack([partner_of(me_ctx, block, ctx_size) for block in range(ctx_size)]).astype(jnp.int32)
    relative_targets = jnp.arange(head_size, dtype=jnp.int32) ^ me_head
    wanted_blocks = (relative_targets[:, None] * per_target + jnp.arange(per_target, dtype=jnp.int32)[None, :]).reshape(-1)
    ordered = jnp.take(out_blocks, slot_of_block[wanted_blocks], axis=0)
    ordered = ordered.reshape(head_size, per_target * rows_here, heads_here * V_DIM)
    partials = jnp.einsum("trf,fc->trc", ordered, w_out, preferred_element_type=jnp.float32)
    if partials.shape[-1] % 256 == 0:
        half = partials.shape[-1] // 2
        total = jnp.concatenate(
            [reduce_scatter_head(partials[..., :half], head_size), reduce_scatter_head(partials[..., half:], head_size)],
            axis=-1,
        )
    else:
        total = reduce_scatter_head(partials, head_size)
    return total.astype(jnp.bfloat16)


def solution(mesh):
    placed = (
        P(("grp", "ctx"), "head"),
        P(("grp", "ctx"), None),
        P(None, "head"),
        P("head", "ctx"),
        P("grp"),
    )
    body = lambda *args: on_device(*args, ctx_size=mesh.shape["ctx"], head_size=mesh.shape["head"])
    return jax.shard_map(
        body, mesh=mesh, in_specs=placed, out_specs=P(("grp", "head"), "ctx"), check_vma=False
    )
```

```python
import math

import jax
import jax.numpy as jnp
from jax import lax
from jax.sharding import PartitionSpec as P

LATENT = 256
ROPE = 64
HEAD_DIM = 64
V_DIM = 64

NEGATIVE = -1e30
DIRECT_LIMIT = 8


def positions_of(block_order, global_rows, half_rows):
    block_index = global_rows // half_rows
    matches = block_index[:, None] == jnp.arange(block_order.shape[0], dtype=jnp.int32)[None, :]
    picked = jnp.sum(jnp.where(matches, block_order[None, :], 0), axis=1)
    return picked * half_rows + global_rows % half_rows


def gather_ctx(x, ctx_size, relay=False):
    me = lax.axis_index("ctx")
    if ctx_size > DIRECT_LIMIT:
        whole = lax.all_gather(x, "ctx", axis=0, tiled=False)
        return whole, jnp.arange(ctx_size, dtype=jnp.int32)
    if relay and ctx_size == 4:
        near = lax.ppermute(x, "ctx", [(i ^ 1, i) for i in range(4)])
        far = lax.ppermute(x, "ctx", [(i ^ 2, i) for i in range(4)])
        relayed = lax.ppermute(far, "ctx", [(i ^ 1, i) for i in range(4)])
        sources = me ^ jnp.arange(4, dtype=jnp.int32)
        return jnp.stack([x, near, far, relayed]), sources
    pieces = [x]
    for step in range(1, ctx_size):
        pairs = [(partner_of(i, step, ctx_size), i) for i in range(ctx_size)]
        pieces.append(lax.ppermute(x, "ctx", pairs))
    sources = jnp.stack([partner_of(me, step, ctx_size) for step in range(ctx_size)]).astype(jnp.int32)
    return jnp.stack(pieces), sources


def partner_of(i, step, size):
    if size & (size - 1) == 0:
        return i ^ step
    return (i - step) % size


def reduce_scatter_head(relative, head_size):
    acc = relative
    bit = 1
    while bit < head_size:
        pairs = [(i, i ^ bit) for i in range(head_size)]
        grouped = acc.reshape((acc.shape[0] // 2, 2) + acc.shape[1:])
        kept = grouped[:, 0]
        sent = grouped[:, 1].astype(jnp.bfloat16)
        got = lax.ppermute(sent, "head", pairs)
        acc = kept + got.astype(jnp.float32)
        bit *= 2
    return acc[0]


def on_device(queries, latents, w_kv_up, w_out, block_order, *, ctx_size, head_size):
    rows_here = queries.shape[0]
    half_rows = rows_here // 2
    width_qk = HEAD_DIM + ROPE
    width_kv = HEAD_DIM + V_DIM
    heads_here = w_kv_up.shape[1] // width_kv
    scaling = 1.0 / math.sqrt(width_qk)
    highest_p = lax.Precision.HIGHEST
    me_ctx = lax.axis_index("ctx")
    me_head = lax.axis_index("head")

    blocks, sources = gather_ctx(latents, ctx_size)
    piece = blocks.reshape(ctx_size * rows_here, latents.shape[1])
    token_rows = (sources[:, None] * rows_here + jnp.arange(rows_here, dtype=jnp.int32)[None, :]).reshape(-1)

    queries3 = queries.reshape(rows_here, heads_here, width_qk)
    query_nope = queries3[:, :, :HEAD_DIM].astype(jnp.float32)
    query_rope = queries3[:, :, HEAD_DIM:]
    query_rows = me_ctx * rows_here + jnp.arange(rows_here, dtype=jnp.int32)
    query_pos = positions_of(block_order, query_rows, half_rows)

    row_count = piece.shape[0]
    packed = jnp.dot(piece[:, :LATENT], w_kv_up, preferred_element_type=jnp.float32)
    packed = packed.reshape(row_count, heads_here, width_kv)
    scores = jnp.einsum("qhd,khd->qhk", query_nope, packed[:, :, :HEAD_DIM], precision=highest_p)
    scores = scores + jnp.einsum(
        "qhd,kd->qhk", query_rope, piece[:, LATENT:], preferred_element_type=jnp.float32
    )
    scores = scores * scaling
    visible = (positions_of(block_order, token_rows, half_rows)[None, :] <= query_pos[:, None])[:, None, :]
    scores = jnp.where(visible, scores, NEGATIVE)
    highest = jnp.max(scores, axis=2, keepdims=True)
    weights = jnp.where(visible, jnp.exp(scores - highest), 0.0)
    totals = jnp.sum(weights, axis=2, keepdims=True)
    widened = lax.optimization_barrier(weights.astype(jnp.bfloat16)).astype(jnp.float32)
    mixed = jnp.einsum("qhk,khd->qhd", widened, packed[:, :, HEAD_DIM:], precision=highest_p)
    outputs = (mixed / totals).astype(jnp.bfloat16).reshape(rows_here, heads_here * V_DIM)

    out_blocks, out_sources = gather_ctx(outputs, ctx_size, relay=True)
    per_target = ctx_size // head_size
    if ctx_size > DIRECT_LIMIT:
        slot_of_block = jnp.arange(ctx_size, dtype=jnp.int32)
    else:
        slot_of_block = jnp.stack([partner_of(me_ctx, block, ctx_size) for block in range(ctx_size)]).astype(jnp.int32)
    relative_targets = jnp.arange(head_size, dtype=jnp.int32) ^ me_head
    wanted_blocks = (relative_targets[:, None] * per_target + jnp.arange(per_target, dtype=jnp.int32)[None, :]).reshape(-1)
    ordered = jnp.take(out_blocks, slot_of_block[wanted_blocks], axis=0)
    ordered = ordered.reshape(head_size, per_target * rows_here, heads_here * V_DIM)
    if w_out.shape[-1] % 256 == 0:
        half = w_out.shape[-1] // 2
        chains = []
        for columns in (slice(0, half), slice(half, None)):
            partials = jnp.einsum("trf,fc->trc", ordered, w_out[:, columns], preferred_element_type=jnp.float32)
            chains.append(reduce_scatter_head(partials, head_size))
        total = jnp.concatenate(chains, axis=-1)
    else:
        partials = jnp.einsum("trf,fc->trc", ordered, w_out, preferred_element_type=jnp.float32)
        total = reduce_scatter_head(partials, head_size)
    return total.astype(jnp.bfloat16)


def solution(mesh):
    placed = (
        P(("grp", "ctx"), "head"),
        P(("grp", "ctx"), None),
        P(None, "head"),
        P("head", "ctx"),
        P("grp"),
    )
    body = lambda *args: on_device(*args, ctx_size=mesh.shape["ctx"], head_size=mesh.shape["head"])
    return jax.shard_map(
        body, mesh=mesh, in_specs=placed, out_specs=P(("grp", "head"), "ctx"), check_vma=False
    )
```

```python
import math

import jax
import jax.numpy as jnp
from jax import lax
from jax.sharding import PartitionSpec as P

LATENT = 256
ROPE = 64
HEAD_DIM = 64
V_DIM = 64

NEGATIVE = -1e30
DIRECT_LIMIT = 8
CHAINS = 4


def positions_of(block_order, global_rows, half_rows):
    block_index = global_rows // half_rows
    matches = block_index[:, None] == jnp.arange(block_order.shape[0], dtype=jnp.int32)[None, :]
    picked = jnp.sum(jnp.where(matches, block_order[None, :], 0), axis=1)
    return picked * half_rows + global_rows % half_rows


def gather_ctx(x, ctx_size, relay=False):
    me = lax.axis_index("ctx")
    if ctx_size > DIRECT_LIMIT:
        whole = lax.all_gather(x, "ctx", axis=0, tiled=False)
        return whole, jnp.arange(ctx_size, dtype=jnp.int32)
    if relay and ctx_size == 4:
        near = lax.ppermute(x, "ctx", [(i ^ 1, i) for i in range(4)])
        far = lax.ppermute(x, "ctx", [(i ^ 2, i) for i in range(4)])
        relayed = lax.ppermute(far, "ctx", [(i ^ 1, i) for i in range(4)])
        sources = me ^ jnp.arange(4, dtype=jnp.int32)
        return jnp.stack([x, near, far, relayed]), sources
    pieces = [x]
    for step in range(1, ctx_size):
        pairs = [(partner_of(i, step, ctx_size), i) for i in range(ctx_size)]
        pieces.append(lax.ppermute(x, "ctx", pairs))
    sources = jnp.stack([partner_of(me, step, ctx_size) for step in range(ctx_size)]).astype(jnp.int32)
    return jnp.stack(pieces), sources


def partner_of(i, step, size):
    if size & (size - 1) == 0:
        return i ^ step
    return (i - step) % size


def reduce_scatter_head(relative, head_size):
    acc = relative
    bit = 1
    while bit < head_size:
        pairs = [(i, i ^ bit) for i in range(head_size)]
        grouped = acc.reshape((acc.shape[0] // 2, 2) + acc.shape[1:])
        kept = grouped[:, 0]
        sent = grouped[:, 1].astype(jnp.bfloat16)
        got = lax.ppermute(sent, "head", pairs)
        acc = kept + got.astype(jnp.float32)
        bit *= 2
    return acc[0]


def on_device(queries, latents, w_kv_up, w_out, block_order, *, ctx_size, head_size):
    rows_here = queries.shape[0]
    half_rows = rows_here // 2
    width_qk = HEAD_DIM + ROPE
    width_kv = HEAD_DIM + V_DIM
    heads_here = w_kv_up.shape[1] // width_kv
    scaling = 1.0 / math.sqrt(width_qk)
    highest_p = lax.Precision.HIGHEST
    me_ctx = lax.axis_index("ctx")
    me_head = lax.axis_index("head")

    blocks, sources = gather_ctx(latents, ctx_size)
    piece = blocks.reshape(ctx_size * rows_here, latents.shape[1])
    token_rows = (sources[:, None] * rows_here + jnp.arange(rows_here, dtype=jnp.int32)[None, :]).reshape(-1)

    queries3 = queries.reshape(rows_here, heads_here, width_qk)
    query_nope = queries3[:, :, :HEAD_DIM].astype(jnp.float32)
    query_rope = queries3[:, :, HEAD_DIM:]
    query_rows = me_ctx * rows_here + jnp.arange(rows_here, dtype=jnp.int32)
    query_pos = positions_of(block_order, query_rows, half_rows)

    row_count = piece.shape[0]
    packed = jnp.dot(piece[:, :LATENT], w_kv_up, preferred_element_type=jnp.float32)
    packed = packed.reshape(row_count, heads_here, width_kv)
    scores = jnp.einsum("qhd,khd->qhk", query_nope, packed[:, :, :HEAD_DIM], precision=highest_p)
    scores = scores + jnp.einsum(
        "qhd,kd->qhk", query_rope, piece[:, LATENT:], preferred_element_type=jnp.float32
    )
    scores = scores * scaling
    visible = (positions_of(block_order, token_rows, half_rows)[None, :] <= query_pos[:, None])[:, None, :]
    scores = jnp.where(visible, scores, NEGATIVE)
    highest = jnp.max(scores, axis=2, keepdims=True)
    weights = jnp.where(visible, jnp.exp(scores - highest), 0.0)
    totals = jnp.sum(weights, axis=2, keepdims=True)
    widened = lax.optimization_barrier(weights.astype(jnp.bfloat16)).astype(jnp.float32)
    mixed = jnp.einsum("qhk,khd->qhd", widened, packed[:, :, HEAD_DIM:], precision=highest_p)
    outputs = (mixed / totals).astype(jnp.bfloat16).reshape(rows_here, heads_here * V_DIM)

    out_blocks, out_sources = gather_ctx(outputs, ctx_size, relay=True)
    per_target = ctx_size // head_size
    if ctx_size > DIRECT_LIMIT:
        slot_of_block = jnp.arange(ctx_size, dtype=jnp.int32)
    else:
        slot_of_block = jnp.stack([partner_of(me_ctx, block, ctx_size) for block in range(ctx_size)]).astype(jnp.int32)
    relative_targets = jnp.arange(head_size, dtype=jnp.int32) ^ me_head
    wanted_blocks = (relative_targets[:, None] * per_target + jnp.arange(per_target, dtype=jnp.int32)[None, :]).reshape(-1)
    ordered = jnp.take(out_blocks, slot_of_block[wanted_blocks], axis=0)
    ordered = ordered.reshape(head_size, per_target * rows_here, heads_here * V_DIM)
    partials = jnp.einsum("trf,fc->trc", ordered, w_out, preferred_element_type=jnp.float32)
    if partials.shape[-1] % 256 == 0:
        lanes = partials.shape[-1] // 128
        cuts = [128 * ((lanes * k) // CHAINS) for k in range(CHAINS + 1)]
        total = jnp.concatenate(
            [reduce_scatter_head(partials[..., lo:hi], head_size) for lo, hi in zip(cuts[:-1], cuts[1:]) if hi > lo],
            axis=-1,
        )
    else:
        total = reduce_scatter_head(partials, head_size)
    return total.astype(jnp.bfloat16)


def solution(mesh):
    placed = (
        P(("grp", "ctx"), "head"),
        P(("grp", "ctx"), None),
        P(None, "head"),
        P("head", "ctx"),
        P("grp"),
    )
    body = lambda *args: on_device(*args, ctx_size=mesh.shape["ctx"], head_size=mesh.shape["head"])
    return jax.shard_map(
        body, mesh=mesh, in_specs=placed, out_specs=P(("grp", "head"), "ctx"), check_vma=False
    )
```

```python
import math

import jax
import jax.numpy as jnp
from jax import lax
from jax.sharding import PartitionSpec as P

LATENT = 256
ROPE = 64
HEAD_DIM = 64
V_DIM = 64

NEGATIVE = -1e30
DIRECT_LIMIT = 8


def positions_of(block_order, global_rows, half_rows):
    block_index = global_rows // half_rows
    matches = block_index[:, None] == jnp.arange(block_order.shape[0], dtype=jnp.int32)[None, :]
    picked = jnp.sum(jnp.where(matches, block_order[None, :], 0), axis=1)
    return picked * half_rows + global_rows % half_rows


def gather_ctx(x, ctx_size, relay=False):
    me = lax.axis_index("ctx")
    if ctx_size > DIRECT_LIMIT:
        whole = lax.all_gather(x, "ctx", axis=0, tiled=False)
        return whole, jnp.arange(ctx_size, dtype=jnp.int32)
    if relay and ctx_size == 4:
        near = lax.ppermute(x, "ctx", [(i ^ 1, i) for i in range(4)])
        far = lax.ppermute(x, "ctx", [(i ^ 2, i) for i in range(4)])
        relayed = lax.ppermute(far, "ctx", [(i ^ 1, i) for i in range(4)])
        sources = me ^ jnp.arange(4, dtype=jnp.int32)
        return jnp.stack([x, near, far, relayed]), sources
    pieces = [x]
    for step in range(1, ctx_size):
        pairs = [(partner_of(i, step, ctx_size), i) for i in range(ctx_size)]
        pieces.append(lax.ppermute(x, "ctx", pairs))
    sources = jnp.stack([partner_of(me, step, ctx_size) for step in range(ctx_size)]).astype(jnp.int32)
    return jnp.stack(pieces), sources


def partner_of(i, step, size):
    if size & (size - 1) == 0:
        return i ^ step
    return (i - step) % size


def reduce_scatter_head(relative, head_size):
    acc = relative
    bit = 1
    while bit < head_size:
        pairs = [(i, i ^ bit) for i in range(head_size)]
        grouped = acc.reshape((acc.shape[0] // 2, 2) + acc.shape[1:])
        kept = grouped[:, 0]
        sent = grouped[:, 1].astype(jnp.bfloat16)
        got = lax.ppermute(sent, "head", pairs)
        acc = kept + got.astype(jnp.float32)
        bit *= 2
    return acc[0]


def on_device(queries, latents, w_kv_up, w_out, block_order, *, ctx_size, head_size):
    rows_here = queries.shape[0]
    half_rows = rows_here // 2
    width_qk = HEAD_DIM + ROPE
    width_kv = HEAD_DIM + V_DIM
    heads_here = w_kv_up.shape[1] // width_kv
    scaling = 1.0 / math.sqrt(width_qk)
    highest_p = lax.Precision.HIGHEST
    me_ctx = lax.axis_index("ctx")
    me_head = lax.axis_index("head")

    blocks, sources = gather_ctx(latents, ctx_size)
    piece = blocks.reshape(ctx_size * rows_here, latents.shape[1])
    token_rows = (sources[:, None] * rows_here + jnp.arange(rows_here, dtype=jnp.int32)[None, :]).reshape(-1)

    queries3 = queries.reshape(rows_here, heads_here, width_qk)
    query_nope = queries3[:, :, :HEAD_DIM].astype(jnp.float32)
    query_rope = queries3[:, :, HEAD_DIM:]
    query_rows = me_ctx * rows_here + jnp.arange(rows_here, dtype=jnp.int32)
    query_pos = positions_of(block_order, query_rows, half_rows)

    row_count = piece.shape[0]
    packed = jnp.dot(piece[:, :LATENT], w_kv_up, preferred_element_type=jnp.float32)
    packed = packed.reshape(row_count, heads_here, width_kv)
    scores = jnp.einsum("qhd,khd->qhk", query_nope, packed[:, :, :HEAD_DIM], precision=highest_p)
    scores = scores + jnp.einsum(
        "qhd,kd->qhk", query_rope, piece[:, LATENT:], preferred_element_type=jnp.float32
    )
    scores = scores * scaling
    visible = (positions_of(block_order, token_rows, half_rows)[None, :] <= query_pos[:, None])[:, None, :]
    scores = jnp.where(visible, scores, NEGATIVE)
    highest = jnp.max(scores, axis=2, keepdims=True)
    weights = jnp.where(visible, jnp.exp(scores - highest), 0.0)
    totals = jnp.sum(weights, axis=2, keepdims=True)
    widened = lax.optimization_barrier(weights.astype(jnp.bfloat16)).astype(jnp.float32)
    mixed = jnp.einsum("qhk,khd->qhd", widened, packed[:, :, HEAD_DIM:], precision=highest_p)
    outputs = (mixed / totals).astype(jnp.bfloat16).reshape(rows_here, heads_here * V_DIM)

    out_blocks, out_sources = gather_ctx(outputs, ctx_size)
    per_target = ctx_size // head_size
    if ctx_size > DIRECT_LIMIT:
        slot_of_block = jnp.arange(ctx_size, dtype=jnp.int32)
    else:
        slot_of_block = jnp.stack([partner_of(me_ctx, block, ctx_size) for block in range(ctx_size)]).astype(jnp.int32)
    relative_targets = jnp.arange(head_size, dtype=jnp.int32) ^ me_head
    wanted_blocks = (relative_targets[:, None] * per_target + jnp.arange(per_target, dtype=jnp.int32)[None, :]).reshape(-1)
    ordered = jnp.take(out_blocks, slot_of_block[wanted_blocks], axis=0)
    ordered = ordered.reshape(head_size, per_target * rows_here, heads_here * V_DIM)
    partials = jnp.einsum("trf,fc->trc", ordered, w_out, preferred_element_type=jnp.float32)
    if partials.shape[-1] % 256 == 0:
        half = partials.shape[-1] // 2
        total = jnp.concatenate(
            [reduce_scatter_head(partials[..., :half], head_size), reduce_scatter_head(partials[..., half:], head_size)],
            axis=-1,
        )
    else:
        total = reduce_scatter_head(partials, head_size)
    return total.astype(jnp.bfloat16)


def solution(mesh):
    placed = (
        P(("grp", "ctx"), "head"),
        P(("grp", "ctx"), None),
        P(None, "head"),
        P("head", "ctx"),
        P("grp"),
    )
    body = lambda *args: on_device(*args, ctx_size=mesh.shape["ctx"], head_size=mesh.shape["head"])
    return jax.shard_map(
        body, mesh=mesh, in_specs=placed, out_specs=P(("grp", "head"), "ctx"), check_vma=False
    )
```

```python
import math

import jax
import jax.numpy as jnp
from jax import lax
from jax.sharding import PartitionSpec as P

LATENT = 256
ROPE = 64
HEAD_DIM = 64
V_DIM = 64

NEGATIVE = -1e30
DIRECT_LIMIT = 8


def positions_of(block_order, global_rows, half_rows):
    block_index = global_rows // half_rows
    matches = block_index[:, None] == jnp.arange(block_order.shape[0], dtype=jnp.int32)[None, :]
    picked = jnp.sum(jnp.where(matches, block_order[None, :], 0), axis=1)
    return picked * half_rows + global_rows % half_rows


def gather_ctx(x, ctx_size, relay=False):
    me = lax.axis_index("ctx")
    if ctx_size > DIRECT_LIMIT:
        whole = lax.all_gather(x, "ctx", axis=0, tiled=False)
        return whole, jnp.arange(ctx_size, dtype=jnp.int32)
    if relay and ctx_size == 4:
        near = lax.ppermute(x, "ctx", [(i ^ 1, i) for i in range(4)])
        far = lax.ppermute(x, "ctx", [(i ^ 2, i) for i in range(4)])
        relayed = lax.ppermute(far, "ctx", [(i ^ 1, i) for i in range(4)])
        sources = me ^ jnp.arange(4, dtype=jnp.int32)
        return jnp.stack([x, near, far, relayed]), sources
    pieces = [x]
    for step in range(1, ctx_size):
        pairs = [(partner_of(i, step, ctx_size), i) for i in range(ctx_size)]
        pieces.append(lax.ppermute(x, "ctx", pairs))
    sources = jnp.stack([partner_of(me, step, ctx_size) for step in range(ctx_size)]).astype(jnp.int32)
    return jnp.stack(pieces), sources


def partner_of(i, step, size):
    if size & (size - 1) == 0:
        return i ^ step
    return (i - step) % size


def reduce_scatter_head(relative, head_size):
    acc = relative
    bit = 1
    while bit < head_size:
        pairs = [(i, i ^ bit) for i in range(head_size)]
        grouped = acc.reshape((acc.shape[0] // 2, 2) + acc.shape[1:])
        kept = grouped[:, 0]
        sent = grouped[:, 1].astype(jnp.bfloat16)
        got = lax.ppermute(sent, "head", pairs)
        acc = kept + got.astype(jnp.float32)
        bit *= 2
    return acc[0]


def on_device(queries, latents, w_kv_up, w_out, block_order, *, ctx_size, head_size):
    rows_here = queries.shape[0]
    half_rows = rows_here // 2
    width_qk = HEAD_DIM + ROPE
    width_kv = HEAD_DIM + V_DIM
    heads_here = w_kv_up.shape[1] // width_kv
    scaling = 1.0 / math.sqrt(width_qk)
    highest_p = lax.Precision.HIGHEST
    me_ctx = lax.axis_index("ctx")
    me_head = lax.axis_index("head")

    blocks, sources = gather_ctx(latents, ctx_size)
    piece = blocks.reshape(ctx_size * rows_here, latents.shape[1])
    token_rows = (sources[:, None] * rows_here + jnp.arange(rows_here, dtype=jnp.int32)[None, :]).reshape(-1)

    queries3 = queries.reshape(rows_here, heads_here, width_qk)
    query_nope = queries3[:, :, :HEAD_DIM].astype(jnp.float32)
    query_rope = queries3[:, :, HEAD_DIM:]
    query_rows = me_ctx * rows_here + jnp.arange(rows_here, dtype=jnp.int32)
    query_pos = positions_of(block_order, query_rows, half_rows)

    row_count = piece.shape[0]
    packed = jnp.dot(piece[:, :LATENT], w_kv_up, preferred_element_type=jnp.float32)
    packed = packed.reshape(row_count, heads_here, width_kv)
    scores = jnp.einsum("qhd,khd->qhk", query_nope, packed[:, :, :HEAD_DIM], precision=highest_p)
    scores = scores + jnp.einsum(
        "qhd,kd->qhk", query_rope, piece[:, LATENT:], preferred_element_type=jnp.float32
    )
    scores = scores * scaling
    visible = (positions_of(block_order, token_rows, half_rows)[None, :] <= query_pos[:, None])[:, None, :]
    scores = jnp.where(visible, scores, NEGATIVE)
    highest = jnp.max(scores, axis=2, keepdims=True)
    weights = jnp.where(visible, jnp.exp(scores - highest), 0.0)
    totals = jnp.sum(weights, axis=2, keepdims=True)
    widened = lax.optimization_barrier(weights.astype(jnp.bfloat16)).astype(jnp.float32)
    mixed = jnp.einsum("qhk,khd->qhd", widened, packed[:, :, HEAD_DIM:], precision=highest_p)
    outputs = (mixed / totals).astype(jnp.bfloat16).reshape(rows_here, heads_here * V_DIM)

    out_blocks, out_sources = gather_ctx(outputs, ctx_size, relay=True)
    per_target = ctx_size // head_size
    if ctx_size > DIRECT_LIMIT:
        slot_of_block = jnp.arange(ctx_size, dtype=jnp.int32)
    else:
        slot_of_block = jnp.stack([partner_of(me_ctx, block, ctx_size) for block in range(ctx_size)]).astype(jnp.int32)
    relative_targets = jnp.arange(head_size, dtype=jnp.int32) ^ me_head
    wanted_blocks = (relative_targets[:, None] * per_target + jnp.arange(per_target, dtype=jnp.int32)[None, :]).reshape(-1)
    ordered = jnp.take(out_blocks, slot_of_block[wanted_blocks], axis=0)
    ordered = ordered.reshape(head_size, per_target * rows_here, heads_here * V_DIM)
    partials = jnp.einsum("trf,fc->trc", ordered, w_out, preferred_element_type=jnp.float32)
    if partials.shape[-1] % 256 == 0:
        half = 128 * max(1, (partials.shape[-1] // 128) * 3 // 7)
        total = jnp.concatenate(
            [reduce_scatter_head(partials[..., :half], head_size), reduce_scatter_head(partials[..., half:], head_size)],
            axis=-1,
        )
    else:
        total = reduce_scatter_head(partials, head_size)
    return total.astype(jnp.bfloat16)


def solution(mesh):
    placed = (
        P(("grp", "ctx"), "head"),
        P(("grp", "ctx"), None),
        P(None, "head"),
        P("head", "ctx"),
        P("grp"),
    )
    body = lambda *args: on_device(*args, ctx_size=mesh.shape["ctx"], head_size=mesh.shape["head"])
    return jax.shard_map(
        body, mesh=mesh, in_specs=placed, out_specs=P(("grp", "head"), "ctx"), check_vma=False
    )
```

```python
import math

import jax
import jax.numpy as jnp
from jax import lax
from jax.sharding import PartitionSpec as P

LATENT = 256
ROPE = 64
HEAD_DIM = 64
V_DIM = 64

NEGATIVE = -1e30
DIRECT_LIMIT = 8


def positions_of(block_order, global_rows, half_rows):
    block_index = global_rows // half_rows
    matches = block_index[:, None] == jnp.arange(block_order.shape[0], dtype=jnp.int32)[None, :]
    picked = jnp.sum(jnp.where(matches, block_order[None, :], 0), axis=1)
    return picked * half_rows + global_rows % half_rows


def gather_ctx(x, ctx_size, relay=False):
    me = lax.axis_index("ctx")
    if ctx_size > DIRECT_LIMIT:
        whole = lax.all_gather(x, "ctx", axis=0, tiled=False)
        return whole, jnp.arange(ctx_size, dtype=jnp.int32)
    if relay and ctx_size == 4:
        near = lax.ppermute(x, "ctx", [(i ^ 1, i) for i in range(4)])
        far = lax.ppermute(x, "ctx", [(i ^ 2, i) for i in range(4)])
        relayed = lax.ppermute(far, "ctx", [(i ^ 1, i) for i in range(4)])
        sources = me ^ jnp.arange(4, dtype=jnp.int32)
        return jnp.stack([x, near, far, relayed]), sources
    pieces = [x]
    for step in range(1, ctx_size):
        pairs = [(partner_of(i, step, ctx_size), i) for i in range(ctx_size)]
        pieces.append(lax.ppermute(x, "ctx", pairs))
    sources = jnp.stack([partner_of(me, step, ctx_size) for step in range(ctx_size)]).astype(jnp.int32)
    return jnp.stack(pieces), sources


def partner_of(i, step, size):
    if size & (size - 1) == 0:
        return i ^ step
    return (i - step) % size


def reduce_scatter_head(relative, head_size):
    acc = relative
    bit = 1
    while bit < head_size:
        pairs = [(i, i ^ bit) for i in range(head_size)]
        grouped = acc.reshape((acc.shape[0] // 2, 2) + acc.shape[1:])
        kept = grouped[:, 0]
        sent = grouped[:, 1].astype(jnp.bfloat16)
        got = lax.ppermute(sent, "head", pairs)
        acc = kept + got.astype(jnp.float32)
        bit *= 2
    return acc[0]


def on_device(queries, latents, w_kv_up, w_out, block_order, *, ctx_size, head_size):
    rows_here = queries.shape[0]
    half_rows = rows_here // 2
    width_qk = HEAD_DIM + ROPE
    width_kv = HEAD_DIM + V_DIM
    heads_here = w_kv_up.shape[1] // width_kv
    scaling = 1.0 / math.sqrt(width_qk)
    highest_p = lax.Precision.HIGHEST
    me_ctx = lax.axis_index("ctx")
    me_head = lax.axis_index("head")

    blocks, sources = gather_ctx(latents, ctx_size)
    piece = blocks.reshape(ctx_size * rows_here, latents.shape[1])
    token_rows = (sources[:, None] * rows_here + jnp.arange(rows_here, dtype=jnp.int32)[None, :]).reshape(-1)

    queries3 = queries.reshape(rows_here, heads_here, width_qk)
    query_nope = queries3[:, :, :HEAD_DIM].astype(jnp.float32)
    query_rope = queries3[:, :, HEAD_DIM:]
    query_rows = me_ctx * rows_here + jnp.arange(rows_here, dtype=jnp.int32)
    query_pos = positions_of(block_order, query_rows, half_rows)

    row_count = piece.shape[0]
    packed = jnp.dot(piece[:, :LATENT], w_kv_up, preferred_element_type=jnp.float32)
    packed = packed.reshape(row_count, heads_here, width_kv)
    scores = jnp.einsum("qhd,khd->qhk", query_nope, packed[:, :, :HEAD_DIM], precision=highest_p)
    scores = scores + jnp.einsum(
        "qhd,kd->qhk", query_rope, piece[:, LATENT:], preferred_element_type=jnp.float32
    )
    scores = scores * scaling
    visible = (positions_of(block_order, token_rows, half_rows)[None, :] <= query_pos[:, None])[:, None, :]
    scores = jnp.where(visible, scores, NEGATIVE)
    highest = jnp.max(scores, axis=2, keepdims=True)
    weights = jnp.where(visible, jnp.exp(scores - highest), 0.0)
    totals = jnp.sum(weights, axis=2, keepdims=True)
    widened = lax.optimization_barrier(weights.astype(jnp.bfloat16)).astype(jnp.float32)
    mixed = jnp.einsum("qhk,khd->qhd", widened, packed[:, :, HEAD_DIM:], precision=highest_p)
    outputs = (mixed / totals).astype(jnp.bfloat16).reshape(rows_here, heads_here * V_DIM)

    out_blocks, out_sources = gather_ctx(outputs, ctx_size, relay=True)
    per_target = ctx_size // head_size
    if ctx_size > DIRECT_LIMIT:
        slot_of_block = jnp.arange(ctx_size, dtype=jnp.int32)
    else:
        slot_of_block = jnp.stack([partner_of(me_ctx, block, ctx_size) for block in range(ctx_size)]).astype(jnp.int32)
    relative_targets = jnp.arange(head_size, dtype=jnp.int32) ^ me_head
    wanted_blocks = (relative_targets[:, None] * per_target + jnp.arange(per_target, dtype=jnp.int32)[None, :]).reshape(-1)
    ordered = jnp.take(out_blocks, slot_of_block[wanted_blocks], axis=0)
    ordered = ordered.reshape(head_size, per_target * rows_here, heads_here * V_DIM)
    partials = jnp.einsum("trf,fc->trc", ordered, w_out, preferred_element_type=jnp.float32)
    if partials.shape[-1] % 256 == 0:
        half = 128 * max(1, (partials.shape[-1] // 128) * 3 // 14)
        total = jnp.concatenate(
            [reduce_scatter_head(partials[..., :half], head_size), reduce_scatter_head(partials[..., half:], head_size)],
            axis=-1,
        )
    else:
        total = reduce_scatter_head(partials, head_size)
    return total.astype(jnp.bfloat16)


def solution(mesh):
    placed = (
        P(("grp", "ctx"), "head"),
        P(("grp", "ctx"), None),
        P(None, "head"),
        P("head", "ctx"),
        P("grp"),
    )
    body = lambda *args: on_device(*args, ctx_size=mesh.shape["ctx"], head_size=mesh.shape["head"])
    return jax.shard_map(
        body, mesh=mesh, in_specs=placed, out_specs=P(("grp", "head"), "ctx"), check_vma=False
    )
```

```python
import math

import jax
import jax.numpy as jnp
from jax import lax
from jax.sharding import PartitionSpec as P

LATENT = 256
ROPE = 64
HEAD_DIM = 64
V_DIM = 64

NEGATIVE = -1e30
DIRECT_LIMIT = 8


def positions_of(block_order, global_rows, half_rows):
    block_index = global_rows // half_rows
    matches = block_index[:, None] == jnp.arange(block_order.shape[0], dtype=jnp.int32)[None, :]
    picked = jnp.sum(jnp.where(matches, block_order[None, :], 0), axis=1)
    return picked * half_rows + global_rows % half_rows


def gather_ctx(x, ctx_size, relay=False):
    me = lax.axis_index("ctx")
    if ctx_size > DIRECT_LIMIT:
        whole = lax.all_gather(x, "ctx", axis=0, tiled=False)
        return whole, jnp.arange(ctx_size, dtype=jnp.int32)
    if relay and ctx_size == 4:
        near = lax.ppermute(x, "ctx", [(i ^ 1, i) for i in range(4)])
        far = lax.ppermute(x, "ctx", [(i ^ 2, i) for i in range(4)])
        relayed = lax.ppermute(far, "ctx", [(i ^ 1, i) for i in range(4)])
        sources = me ^ jnp.arange(4, dtype=jnp.int32)
        return jnp.stack([x, near, far, relayed]), sources
    pieces = [x]
    for step in range(1, ctx_size):
        pairs = [(partner_of(i, step, ctx_size), i) for i in range(ctx_size)]
        pieces.append(lax.ppermute(x, "ctx", pairs))
    sources = jnp.stack([partner_of(me, step, ctx_size) for step in range(ctx_size)]).astype(jnp.int32)
    return jnp.stack(pieces), sources


def partner_of(i, step, size):
    if size & (size - 1) == 0:
        return i ^ step
    return (i - step) % size


def reduce_scatter_head(relative, head_size):
    acc = relative
    bit = 1
    while bit < head_size:
        pairs = [(i, i ^ bit) for i in range(head_size)]
        grouped = acc.reshape((acc.shape[0] // 2, 2) + acc.shape[1:])
        kept = grouped[:, 0]
        sent = grouped[:, 1].astype(jnp.bfloat16)
        got = lax.ppermute(sent, "head", pairs)
        acc = kept + got.astype(jnp.float32)
        bit *= 2
    return acc[0]


def on_device(queries, latents, w_kv_up, w_out, block_order, *, ctx_size, head_size):
    rows_here = queries.shape[0]
    half_rows = rows_here // 2
    width_qk = HEAD_DIM + ROPE
    width_kv = HEAD_DIM + V_DIM
    heads_here = w_kv_up.shape[1] // width_kv
    scaling = 1.0 / math.sqrt(width_qk)
    highest_p = lax.Precision.HIGHEST
    me_ctx = lax.axis_index("ctx")
    me_head = lax.axis_index("head")

    blocks, sources = gather_ctx(latents, ctx_size)
    piece = blocks.reshape(ctx_size * rows_here, latents.shape[1])
    token_rows = (sources[:, None] * rows_here + jnp.arange(rows_here, dtype=jnp.int32)[None, :]).reshape(-1)

    queries3 = queries.reshape(rows_here, heads_here, width_qk)
    query_nope = queries3[:, :, :HEAD_DIM].astype(jnp.float32)
    query_rope = queries3[:, :, HEAD_DIM:]
    query_rows = me_ctx * rows_here + jnp.arange(rows_here, dtype=jnp.int32)
    query_pos = positions_of(block_order, query_rows, half_rows)

    row_count = piece.shape[0]
    packed = jnp.dot(piece[:, :LATENT], w_kv_up, preferred_element_type=jnp.float32)
    packed = packed.reshape(row_count, heads_here, width_kv)
    scores = jnp.einsum("qhd,khd->qhk", query_nope, packed[:, :, :HEAD_DIM], precision=highest_p)
    scores = scores + jnp.einsum(
        "qhd,kd->qhk", query_rope, piece[:, LATENT:], preferred_element_type=jnp.float32
    )
    scores = scores * scaling
    visible = (positions_of(block_order, token_rows, half_rows)[None, :] <= query_pos[:, None])[:, None, :]
    scores = jnp.where(visible, scores, NEGATIVE)
    highest = jnp.max(scores, axis=2, keepdims=True)
    weights = jnp.where(visible, jnp.exp(scores - highest), 0.0)
    totals = jnp.sum(weights, axis=2, keepdims=True)
    widened = lax.optimization_barrier(weights.astype(jnp.bfloat16)).astype(jnp.float32)
    mixed = jnp.einsum("qhk,khd->qhd", widened, packed[:, :, HEAD_DIM:], precision=highest_p)
    outputs = (mixed / totals).astype(jnp.bfloat16).reshape(rows_here, heads_here * V_DIM)

    out_blocks, out_sources = gather_ctx(outputs, ctx_size, relay=True)
    per_target = ctx_size // head_size
    if ctx_size > DIRECT_LIMIT:
        slot_of_block = jnp.arange(ctx_size, dtype=jnp.int32)
    else:
        slot_of_block = jnp.stack([partner_of(me_ctx, block, ctx_size) for block in range(ctx_size)]).astype(jnp.int32)
    relative_targets = jnp.arange(head_size, dtype=jnp.int32) ^ me_head
    wanted_blocks = (relative_targets[:, None] * per_target + jnp.arange(per_target, dtype=jnp.int32)[None, :]).reshape(-1)
    ordered = jnp.take(out_blocks, slot_of_block[wanted_blocks], axis=0)
    ordered = ordered.reshape(head_size, per_target * rows_here, heads_here * V_DIM)
    partials = jnp.einsum("trf,fc->trc", ordered, w_out, preferred_element_type=jnp.float32)
    if partials.shape[-1] % 256 == 0:
        half = 128 * max(1, (partials.shape[-1] // 128) * 2 // 7)
        total = jnp.concatenate(
            [reduce_scatter_head(partials[..., :half], head_size), reduce_scatter_head(partials[..., half:], head_size)],
            axis=-1,
        )
    else:
        total = reduce_scatter_head(partials, head_size)
    return total.astype(jnp.bfloat16)


def solution(mesh):
    placed = (
        P(("grp", "ctx"), "head"),
        P(("grp", "ctx"), None),
        P(None, "head"),
        P("head", "ctx"),
        P("grp"),
    )
    body = lambda *args: on_device(*args, ctx_size=mesh.shape["ctx"], head_size=mesh.shape["head"])
    return jax.shard_map(
        body, mesh=mesh, in_specs=placed, out_specs=P(("grp", "head"), "ctx"), check_vma=False
    )
```

```python
import math

import jax
import jax.numpy as jnp
from jax import lax
from jax.sharding import PartitionSpec as P

LATENT = 256
ROPE = 64
HEAD_DIM = 64
V_DIM = 64

NEGATIVE = -1e30
DIRECT_LIMIT = 8


def positions_of(block_order, global_rows, half_rows):
    block_index = global_rows // half_rows
    matches = block_index[:, None] == jnp.arange(block_order.shape[0], dtype=jnp.int32)[None, :]
    picked = jnp.sum(jnp.where(matches, block_order[None, :], 0), axis=1)
    return picked * half_rows + global_rows % half_rows


def gather_ctx(x, ctx_size, relay=False):
    me = lax.axis_index("ctx")
    if ctx_size > DIRECT_LIMIT:
        whole = lax.all_gather(x, "ctx", axis=0, tiled=False)
        return whole, jnp.arange(ctx_size, dtype=jnp.int32)
    if relay and ctx_size == 4:
        near = lax.ppermute(x, "ctx", [(i ^ 1, i) for i in range(4)])
        far = lax.ppermute(x, "ctx", [(i ^ 2, i) for i in range(4)])
        relayed = lax.ppermute(far, "ctx", [(i ^ 1, i) for i in range(4)])
        sources = me ^ jnp.arange(4, dtype=jnp.int32)
        return jnp.stack([x, near, far, relayed]), sources
    pieces = [x]
    for step in range(1, ctx_size):
        pairs = [(partner_of(i, step, ctx_size), i) for i in range(ctx_size)]
        pieces.append(lax.ppermute(x, "ctx", pairs))
    sources = jnp.stack([partner_of(me, step, ctx_size) for step in range(ctx_size)]).astype(jnp.int32)
    return jnp.stack(pieces), sources


def partner_of(i, step, size):
    if size & (size - 1) == 0:
        return i ^ step
    return (i - step) % size


def reduce_scatter_head(relative, head_size):
    acc = relative
    bit = 1
    while bit < head_size:
        pairs = [(i, i ^ bit) for i in range(head_size)]
        grouped = acc.reshape((acc.shape[0] // 2, 2) + acc.shape[1:])
        kept = grouped[:, 0]
        sent = grouped[:, 1].astype(jnp.bfloat16)
        got = lax.ppermute(sent, "head", pairs)
        acc = kept + got.astype(jnp.float32)
        bit *= 2
    return acc[0]


def on_device(queries, latents, w_kv_up, w_out, block_order, *, ctx_size, head_size):
    rows_here = queries.shape[0]
    half_rows = rows_here // 2
    width_qk = HEAD_DIM + ROPE
    width_kv = HEAD_DIM + V_DIM
    heads_here = w_kv_up.shape[1] // width_kv
    scaling = 1.0 / math.sqrt(width_qk)
    highest_p = lax.Precision.HIGHEST
    me_ctx = lax.axis_index("ctx")
    me_head = lax.axis_index("head")

    blocks, sources = gather_ctx(latents, ctx_size)
    piece = blocks.reshape(ctx_size * rows_here, latents.shape[1])
    token_rows = (sources[:, None] * rows_here + jnp.arange(rows_here, dtype=jnp.int32)[None, :]).reshape(-1)

    queries3 = queries.reshape(rows_here, heads_here, width_qk)
    query_nope = queries3[:, :, :HEAD_DIM].astype(jnp.float32)
    query_rope = queries3[:, :, HEAD_DIM:]
    query_rows = me_ctx * rows_here + jnp.arange(rows_here, dtype=jnp.int32)
    query_pos = positions_of(block_order, query_rows, half_rows)

    row_count = piece.shape[0]
    packed = jnp.dot(piece[:, :LATENT], w_kv_up, preferred_element_type=jnp.float32)
    packed = packed.reshape(row_count, heads_here, width_kv)
    scores = jnp.einsum("qhd,khd->qhk", query_nope, packed[:, :, :HEAD_DIM], precision=highest_p)
    scores = scores + jnp.einsum(
        "qhd,kd->qhk", query_rope, piece[:, LATENT:], preferred_element_type=jnp.float32
    )
    scores = scores * scaling
    visible = (positions_of(block_order, token_rows, half_rows)[None, :] <= query_pos[:, None])[:, None, :]
    scores = jnp.where(visible, scores, NEGATIVE)
    highest = jnp.max(scores, axis=2, keepdims=True)
    weights = jnp.where(visible, jnp.exp(scores - highest), 0.0)
    totals = jnp.sum(weights, axis=2, keepdims=True)
    widened = lax.optimization_barrier(weights.astype(jnp.bfloat16)).astype(jnp.float32)
    mixed = jnp.einsum("qhk,khd->qhd", widened, packed[:, :, HEAD_DIM:], precision=highest_p)
    outputs = (mixed / totals).astype(jnp.bfloat16).reshape(rows_here, heads_here * V_DIM)

    out_blocks, out_sources = gather_ctx(outputs, ctx_size, relay=True)
    per_target = ctx_size // head_size
    if ctx_size > DIRECT_LIMIT:
        slot_of_block = jnp.arange(ctx_size, dtype=jnp.int32)
    else:
        slot_of_block = jnp.stack([partner_of(me_ctx, block, ctx_size) for block in range(ctx_size)]).astype(jnp.int32)
    relative_targets = jnp.arange(head_size, dtype=jnp.int32) ^ me_head
    wanted_blocks = (relative_targets[:, None] * per_target + jnp.arange(per_target, dtype=jnp.int32)[None, :]).reshape(-1)
    ordered = jnp.take(out_blocks, slot_of_block[wanted_blocks], axis=0)
    ordered = ordered.reshape(head_size, per_target * rows_here, heads_here * V_DIM)
    partials = jnp.einsum("trf,fc->trc", ordered, w_out, preferred_element_type=jnp.float32)
    if partials.shape[-1] % 256 == 0:
        half = 128 * max(1, (partials.shape[-1] // 128) * 4 // 7)
        total = jnp.concatenate(
            [reduce_scatter_head(partials[..., :half], head_size), reduce_scatter_head(partials[..., half:], head_size)],
            axis=-1,
        )
    else:
        total = reduce_scatter_head(partials, head_size)
    return total.astype(jnp.bfloat16)


def solution(mesh):
    placed = (
        P(("grp", "ctx"), "head"),
        P(("grp", "ctx"), None),
        P(None, "head"),
        P("head", "ctx"),
        P("grp"),
    )
    body = lambda *args: on_device(*args, ctx_size=mesh.shape["ctx"], head_size=mesh.shape["head"])
    return jax.shard_map(
        body, mesh=mesh, in_specs=placed, out_specs=P(("grp", "head"), "ctx"), check_vma=False
    )
```

```python
import math

import jax
import jax.numpy as jnp
from jax import lax
from jax.sharding import PartitionSpec as P

LATENT = 256
ROPE = 64
HEAD_DIM = 64
V_DIM = 64

NEGATIVE = -1e30
DIRECT_LIMIT = 8


def positions_of(block_order, global_rows, half_rows):
    block_index = global_rows // half_rows
    matches = block_index[:, None] == jnp.arange(block_order.shape[0], dtype=jnp.int32)[None, :]
    picked = jnp.sum(jnp.where(matches, block_order[None, :], 0), axis=1)
    return picked * half_rows + global_rows % half_rows


def gather_ctx(x, ctx_size, relay=False):
    me = lax.axis_index("ctx")
    if ctx_size > DIRECT_LIMIT:
        whole = lax.all_gather(x, "ctx", axis=0, tiled=False)
        return whole, jnp.arange(ctx_size, dtype=jnp.int32)
    if relay and ctx_size == 4:
        near = lax.ppermute(x, "ctx", [(i ^ 1, i) for i in range(4)])
        far = lax.ppermute(x, "ctx", [(i ^ 2, i) for i in range(4)])
        relayed = lax.ppermute(far, "ctx", [(i ^ 1, i) for i in range(4)])
        sources = me ^ jnp.arange(4, dtype=jnp.int32)
        return jnp.stack([x, near, far, relayed]), sources
    pieces = [x]
    for step in range(1, ctx_size):
        pairs = [(partner_of(i, step, ctx_size), i) for i in range(ctx_size)]
        pieces.append(lax.ppermute(x, "ctx", pairs))
    sources = jnp.stack([partner_of(me, step, ctx_size) for step in range(ctx_size)]).astype(jnp.int32)
    return jnp.stack(pieces), sources


def partner_of(i, step, size):
    if size & (size - 1) == 0:
        return i ^ step
    return (i - step) % size


def reduce_scatter_head(relative, head_size):
    acc = relative
    bit = 1
    while bit < head_size:
        pairs = [(i, i ^ bit) for i in range(head_size)]
        grouped = acc.reshape((acc.shape[0] // 2, 2) + acc.shape[1:])
        kept = grouped[:, 0]
        sent = grouped[:, 1].astype(jnp.bfloat16)
        got = lax.ppermute(sent, "head", pairs)
        acc = kept + got.astype(jnp.float32)
        bit *= 2
    return acc[0]


def on_device(queries, latents, w_kv_up, w_out, block_order, *, ctx_size, head_size):
    rows_here = queries.shape[0]
    half_rows = rows_here // 2
    width_qk = HEAD_DIM + ROPE
    width_kv = HEAD_DIM + V_DIM
    heads_here = w_kv_up.shape[1] // width_kv
    scaling = 1.0 / math.sqrt(width_qk)
    highest_p = lax.Precision.HIGHEST
    me_ctx = lax.axis_index("ctx")
    me_head = lax.axis_index("head")

    blocks, sources = gather_ctx(latents, ctx_size)
    piece = blocks.reshape(ctx_size * rows_here, latents.shape[1])
    token_rows = (sources[:, None] * rows_here + jnp.arange(rows_here, dtype=jnp.int32)[None, :]).reshape(-1)

    queries3 = queries.reshape(rows_here, heads_here, width_qk)
    query_nope = queries3[:, :, :HEAD_DIM].astype(jnp.float32)
    query_rope = queries3[:, :, HEAD_DIM:]
    query_rows = me_ctx * rows_here + jnp.arange(rows_here, dtype=jnp.int32)
    query_pos = positions_of(block_order, query_rows, half_rows)

    row_count = piece.shape[0]
    packed = jnp.dot(piece[:, :LATENT], w_kv_up, preferred_element_type=jnp.float32)
    packed = packed.reshape(row_count, heads_here, width_kv)
    scores = jnp.einsum("qhd,khd->qhk", query_nope, packed[:, :, :HEAD_DIM], precision=highest_p)
    scores = scores + jnp.einsum(
        "qhd,kd->qhk", query_rope, piece[:, LATENT:], preferred_element_type=jnp.float32
    )
    scores = scores * scaling
    visible = (positions_of(block_order, token_rows, half_rows)[None, :] <= query_pos[:, None])[:, None, :]
    scores = jnp.where(visible, scores, NEGATIVE)
    highest = jnp.max(scores, axis=2, keepdims=True)
    weights = jnp.where(visible, jnp.exp(scores - highest), 0.0)
    totals = jnp.sum(weights, axis=2, keepdims=True)
    widened = lax.optimization_barrier(weights.astype(jnp.bfloat16)).astype(jnp.float32)
    mixed = jnp.einsum("qhk,khd->qhd", widened, packed[:, :, HEAD_DIM:], precision=highest_p)
    outputs = (mixed / totals).astype(jnp.bfloat16).reshape(rows_here, heads_here * V_DIM)

    out_blocks, out_sources = gather_ctx(outputs, ctx_size, relay=True)
    per_target = ctx_size // head_size
    if ctx_size > DIRECT_LIMIT:
        slot_of_block = jnp.arange(ctx_size, dtype=jnp.int32)
    else:
        slot_of_block = jnp.stack([partner_of(me_ctx, block, ctx_size) for block in range(ctx_size)]).astype(jnp.int32)
    relative_targets = jnp.arange(head_size, dtype=jnp.int32) ^ me_head
    wanted_blocks = (relative_targets[:, None] * per_target + jnp.arange(per_target, dtype=jnp.int32)[None, :]).reshape(-1)
    ordered = jnp.take(out_blocks, slot_of_block[wanted_blocks], axis=0)
    ordered = ordered.reshape(head_size, per_target * rows_here, heads_here * V_DIM)
    partials = jnp.einsum("trf,fc->trc", ordered, w_out, preferred_element_type=jnp.float32)
    if partials.shape[-1] % 256 == 0:
        half = 128 * max(1, (partials.shape[-1] // 128) * 5 // 14)
        total = jnp.concatenate(
            [reduce_scatter_head(partials[..., :half], head_size), reduce_scatter_head(partials[..., half:], head_size)],
            axis=-1,
        )
    else:
        total = reduce_scatter_head(partials, head_size)
    return total.astype(jnp.bfloat16)


def solution(mesh):
    placed = (
        P(("grp", "ctx"), "head"),
        P(("grp", "ctx"), None),
        P(None, "head"),
        P("head", "ctx"),
        P("grp"),
    )
    body = lambda *args: on_device(*args, ctx_size=mesh.shape["ctx"], head_size=mesh.shape["head"])
    return jax.shard_map(
        body, mesh=mesh, in_specs=placed, out_specs=P(("grp", "head"), "ctx"), check_vma=False
    )
```
